32 devices in a mesh: grp: 2 (over x), seq: 16 (over z, y, core).
Axes of the slice: x: 2, y: 2, z: 4, core: 2. Of those that a mesh axis runs over, the one named last changes fastest.
Arguments:
- queries: bfloat16 [16384, 4096], P(('grp', 'seq')), parts along dimension 0, may hold values from -16 to 16
- keys: bfloat16 [16384, 2048], P(('grp', 'seq')), parts along dimension 0, may hold values from -16 to 16
- values: bfloat16 [16384, 2048], P(('grp', 'seq')), parts along dimension 0, may hold values from -6 to 6
- segment_ids: int32 [16384], P(('grp', 'seq')), parts along dimension 0, may hold values from 0 to 15, never falling along the last dimension, each value on 1 to 2048 neighbouring positions
Outputs:
- attended: bfloat16 [16384, 4096], P(('grp', 'seq')), parts along dimension 0
The draws below stay inside these ranges and needn't reach their ends.
There are 2 independent parts, one for each index of `grp`. The reference program is written for one: setup_inputs(seed, part) draws one part's arguments, and reference() takes and returns one part's arrays. A program takes and returns all parts, laid end to end along the dimension named above; each array names one. Nothing has to cross between parts.
Inputs may be any that keep to these rules, and one draw needn't show every extreme that they name: `segment_ids`: segment ids never fall along the tokens; every document holds 1 to 2048 tokens and one holds exactly 2048.
All inputs are finite; a program needn't handle non-finite values.
Results may differ from the reference program's by a relative error of at most 0.0039.
Values may be sent and summed in bfloat16 or wider, within the bound.
No kernel may reach another device: no remote copies, remote signals or barrier semaphores. Data moves between devices by JAX's collectives and lax.ppermute only.
A program may use at most 128 MiB of HBM per device.

```python
import math
import jax
import jax.numpy as jnp
import numpy as np
from jax import lax

H = 32
KVH = 16
HD = 128
W = 1024
T_DEV = 512
TOKENS = 8192
DOCS = 16
DOC_MOST = 2048


query_scale = 168.0 ** (-0.5)


def planted(key):
    signs = jnp.where(jax.random.bernoulli(jax.random.fold_in(key, 7), 0.5, (HD,)), 1.0, -1.0).astype(jnp.float32)
    dims = jnp.arange(HD)
    low_dims = (dims % (HD // 2) >= HD // 2 - 8).astype(jnp.float32)
    rows = jnp.arange(TOKENS)
    struck = rows % 61 == 37
    struck_next = (rows + 1) % 61 == 37
    strength = 9.5 + 2.0 * (rows // 61 % 4).astype(jnp.float32)
    strength_next = 9.5 + 2.0 * ((rows + 1) // 61 % 4).astype(jnp.float32)
    vector = signs[None, :] * low_dims[None, :] * strength[:, None]
    factor = 1.0 - 2.0 / (query_scale * 16.0 * strength_next * strength_next)
    vector_next = signs[None, :] * low_dims[None, :] * (strength_next * factor)[:, None]
    return (struck, struck_next, vector, vector_next, low_dims)


def draw_queries(key, part):
    struck, struck_next, vector, vector_next, low_dims = planted(key)
    base = jnp.clip(jax.random.normal(jax.random.fold_in(key, 1), (TOKENS, H, HD), jnp.float32), -6.0, 6.0)
    return base.reshape(TOKENS, H * HD).astype(jnp.bfloat16)


def draw_keys(key, part):
    struck, struck_next, vector, vector_next, low_dims = planted(key)
    base = jnp.clip(jax.random.normal(jax.random.fold_in(key, 2), (TOKENS, KVH, HD), jnp.float32), -6.0, 6.0)
    return base.reshape(TOKENS, KVH * HD).astype(jnp.bfloat16)


def level_of(own_key, extent, pieces, low, high):
    loudness = 1.0
    for dim, blocks in pieces:
        draws = jax.random.uniform(jax.random.fold_in(jax.random.fold_in(own_key, 6), dim), (blocks,), jnp.float32, low / len(pieces), high / len(pieces))
        loudness = loudness * jnp.repeat(jnp.exp(draws), extent[dim] // blocks).reshape((-1,) + (1,) * (len(extent) - 1 - dim))
    return loudness


def length_profile(number_of, total, most, lean):
    loads = [(1 << 20) // math.isqrt(standing ** lean) + 1 for standing in range(2, number_of + 1)]
    spare, counts = total - most - (number_of - 1), [1] * (number_of - 1)
    while spare > 0:
        free = [i for i in range(number_of - 1) if counts[i] < most]
        mass, left = sum([loads[i] for i in free]), spare
        for i in free:
            extra = min(most - counts[i], max(1, left * loads[i] // mass), spare)
            counts[i] = counts[i] + extra
            spare = spare - extra
    return np.array([most] + counts)


def uneven(own_key, amount, total, limit, slope):
    if amount == 2:
        one = jax.random.randint(own_key, (), max(1, total - limit), min(limit, total - 1) + 1)
        return jnp.stack([one, total - one])
    tallies = jnp.asarray(length_profile(amount, total, limit, slope), jnp.int32)
    couples = (amount - 1) // 2
    giver, receiver = tallies[1:1 + 2 * couples:2], tallies[2:2 + 2 * couples:2]
    slack = jnp.minimum(giver - 1, limit - receiver)
    passed = jax.random.randint(jax.random.fold_in(own_key, 1), (couples,), 0, 1 << 20) % (slack + 1)
    tallies = tallies.at[1:1 + 2 * couples:2].set(giver - passed).at[2:2 + 2 * couples:2].set(receiver + passed)
    return tallies[jax.random.permutation(jax.random.fold_in(own_key, 2), amount)]


def bell_draw(own_key, extent, width, limit, split=(), kind=jnp.bfloat16):
    loudness = level_of(own_key, extent, split, -0.22, 0.18) if split else 1.0
    entries = jax.random.normal(own_key, extent, jnp.float32) * width * loudness
    return jnp.minimum(jnp.maximum(entries, -limit), limit).astype(kind)


def setup_inputs(seed: int = 0, part: int = 0) -> dict:
    key_of = jax.random.split(jax.random.key(seed), 5)
    part_splits = jax.random.split(jax.random.fold_in(key_of[4], part), 5)
    queries = draw_queries(jax.random.fold_in(jax.random.fold_in(key_of[4], part), 71), part)
    keys = draw_keys(jax.random.fold_in(jax.random.fold_in(key_of[4], part), 71), part)
    values = bell_draw(part_splits[2], (TOKENS, KVH * HD), 1.0, 6.0, ((0, 16),))
    segment_ids = jnp.searchsorted(jnp.cumsum(uneven(part_splits[3], DOCS, TOKENS, DOC_MOST, 2)), jnp.arange(TOKENS), side="right").astype(jnp.int32)
    return {"queries": queries, "keys": keys, "values": values, "segment_ids": segment_ids}


query_scale = 168.0 ** -0.5


def in_document(segment_ids):
    count = segment_ids.shape[0]
    places = jnp.arange(count, dtype=jnp.int32)
    previous = jnp.concatenate([segment_ids[:1], segment_ids[:-1]])
    boundary = (segment_ids != previous) | (places == 0)
    starts = lax.cummax(jnp.where(boundary, places, 0), axis=0)
    return places - starts


def rotate(x, doc_pos):
    half = x.shape[-1] // 2
    freqs = 10000.0 ** (-2.0 * jnp.arange(half, dtype=jnp.float32) / x.shape[-1])
    angles = doc_pos.astype(jnp.float32)[:, None] * freqs[None, :]
    cosine = jnp.concatenate([jnp.cos(angles), jnp.cos(angles)], -1)[:, None, :]
    sine = jnp.concatenate([jnp.sin(angles), jnp.sin(angles)], -1)[:, None, :]
    turned = jnp.concatenate([-x[..., half:], x[..., :half]], -1)
    return x * cosine + turned * sine


def reference(queries, keys, values, segment_ids):
    doc_pos = in_document(segment_ids)
    q_rot = rotate(queries.astype(jnp.float32).reshape(TOKENS, H, HD), doc_pos).astype(jnp.bfloat16)
    q_rot = lax.optimization_barrier(q_rot.reshape(TOKENS, H * HD))
    k_rot = rotate(keys.astype(jnp.float32).reshape(TOKENS, KVH, HD), doc_pos).astype(jnp.bfloat16)
    k_rot = lax.optimization_barrier(k_rot.reshape(TOKENS, KVH * HD))
    k_pad = jnp.concatenate([jnp.zeros((W, KVH * HD), jnp.bfloat16), k_rot], 0)
    v_pad = jnp.concatenate([jnp.zeros((W, KVH * HD), jnp.bfloat16), values], 0)

    def one_block(block_index):
        first = (block_index * T_DEV).astype(jnp.int32)
        query_block = lax.dynamic_slice_in_dim(q_rot, first, T_DEV, 0).astype(jnp.float32).reshape(T_DEV, KVH, 2, HD)
        key_block = lax.dynamic_slice_in_dim(k_pad, first, W + T_DEV, 0).astype(jnp.float32).reshape(W + T_DEV, KVH, HD)
        value_block = lax.dynamic_slice_in_dim(v_pad, first, W + T_DEV, 0).astype(jnp.float32).reshape(W + T_DEV, KVH, HD)
        pos_block = lax.dynamic_slice_in_dim(doc_pos, first, T_DEV, 0)
        q_glob = first + jnp.arange(T_DEV, dtype=jnp.int32)
        k_glob = first - W + jnp.arange(W + T_DEV, dtype=jnp.int32)
        gap = q_glob[:, None] - k_glob[None, :]
        visible = (gap >= 0) & (gap < W) & (gap <= pos_block[:, None])
        scores = jnp.einsum("qhgd,khd->hgqk", query_block, key_block) * query_scale
        scores = jnp.where(visible[None, None], scores, -1e30)
        row_max = jnp.max(scores, axis=-1, keepdims=True)
        weights = jnp.where(visible[None, None], jnp.exp(scores - row_max), 0.0)
        totals = jnp.sum(weights, axis=-1, keepdims=True)
        rounded = lax.optimization_barrier(weights.astype(jnp.bfloat16)).astype(jnp.float32)
        summed = jnp.einsum("hgqk,khd->qhgd", rounded, value_block)
        result = summed / jnp.transpose(totals, (2, 0, 1, 3))
        return result.reshape(T_DEV, H * HD).astype(jnp.bfloat16)

    blocks = lax.map(one_block, jnp.arange(TOKENS // T_DEV, dtype=jnp.int32))
    return blocks.reshape(TOKENS, H * HD)
```

```python
import functools

import jax
import jax.numpy as jnp
from jax import lax
from jax.experimental import pallas as pl
from jax.experimental.pallas import tpu as pltpu
from jax.sharding import PartitionSpec as P

H = 32
KVH = 16
HD = 128
W = 1024


query_scale = 168.0 ** (-0.5)


def passed_along(value, axis, steps):
    count = lax.axis_size(axis)
    first, last = (max(0, -steps), min(count, count - steps))
    return lax.ppermute(value, axis, [(source, source + steps) for source in range(first, last)])


def rope_tables(doc_pos):
    half = HD // 2
    freqs = 10000.0 ** (-2.0 * jnp.arange(half, dtype=jnp.float32) / HD)
    angles = doc_pos.astype(jnp.float32)[:, None] * freqs[None, :]
    cos, sin = jnp.cos(angles), jnp.sin(angles)
    return jnp.concatenate([cos, cos], -1), jnp.concatenate([-sin, sin], -1)


def attend_kernel(pos_ref, cos_ref, sin_ref, q_ref, *refs, rows, hops):
    k_refs = refs[:hops + 1]
    v_refs = refs[hops + 1:2 * hops + 2]
    o_ref = refs[2 * hops + 2]
    span = (hops + 1) * rows
    cos = cos_ref[...]
    sin = sin_ref[...]

    def rot(x, c, s):
        return x * c + pltpu.roll(x, HD // 2, 1) * s

    k = jnp.concatenate([r[...] for r in k_refs], 0).astype(jnp.float32)
    k = rot(k, cos, sin).astype(jnp.bfloat16)
    v = jnp.concatenate([r[...] for r in v_refs], 0)
    qc = cos[span - rows:]
    qs = sin[span - rows:]
    dp = pos_ref[...]
    r = lax.broadcasted_iota(jnp.int32, (rows, span), 0)
    c = lax.broadcasted_iota(jnp.int32, (rows, span), 1)
    gap = (span - rows) + r - c
    vis = (gap >= 0) & (gap < W) & (gap <= dp)
    for g in range(2):
        q = q_ref[:, g * HD:(g + 1) * HD].astype(jnp.float32)
        q = rot(q, qc, qs).astype(jnp.bfloat16)
        s = lax.dot_general(q, k, (((1,), (1,)), ((), ())), preferred_element_type=jnp.float32)
        s = jnp.where(vis, s * query_scale, -1e30)
        m = jnp.max(s, axis=1, keepdims=True)
        w = jnp.where(vis, jnp.exp(s - m), 0.0)
        tot = jnp.sum(w, axis=1, keepdims=True)
        pv = jnp.dot(w.astype(jnp.bfloat16), v, preferred_element_type=jnp.float32)
        o_ref[:, g * HD:(g + 1) * HD] = (pv / tot).astype(jnp.bfloat16)


def local(queries, keys, values, segment_ids):
    rows = queries.shape[0]
    hops = W // rows
    span = (hops + 1) * rows
    shard = lax.axis_index("seq")
    tails = [passed_along((keys, values), "seq", d) for d in range(hops, 0, -1)]
    seg_all = lax.all_gather(segment_ids, "seq", tiled=True)
    total = seg_all.shape[0]
    places = jnp.arange(total, dtype=jnp.int32)
    previous = jnp.concatenate([seg_all[:1], seg_all[:-1]])
    boundary = (seg_all != previous) | (places == 0)
    starts = lax.cummax(jnp.where(boundary, places, 0), axis=0)
    pos_all = jnp.concatenate([jnp.zeros((hops * rows,), jnp.int32), places - starts])
    pos_win = lax.dynamic_slice_in_dim(pos_all, shard * rows, span, 0)
    cos, sin = rope_tables(pos_win)
    pos_q = pos_win[span - rows:].reshape(rows, 1)
    k_list = [t[0] for t in tails] + [keys]
    v_list = [t[1] for t in tails] + [values]
    kv_spec = pl.BlockSpec((rows, HD), lambda h: (0, h))
    full = lambda shape: pl.BlockSpec(shape, lambda h: (0, 0))
    kernel = functools.partial(attend_kernel, rows=rows, hops=hops)
    heads = keys.shape[1] // HD
    return pl.pallas_call(
        kernel,
        grid=(heads,),
        in_specs=[full((rows, 1)), full((span, HD)), full((span, HD)),
                  pl.BlockSpec((rows, 2 * HD), lambda h: (0, h))]
        + [kv_spec] * (2 * hops + 2),
        out_specs=pl.BlockSpec((rows, 2 * HD), lambda h: (0, h)),
        out_shape=jax.ShapeDtypeStruct(queries.shape, jnp.bfloat16),
        compiler_params=pltpu.CompilerParams(dimension_semantics=("arbitrary",)),
    )(pos_q, cos, sin, queries, *k_list, *v_list)


def solution(mesh):
    return jax.shard_map(
        local,
        mesh=mesh,
        in_specs=(
            P(("grp", "seq"), None),
            P(("grp", "seq"), None),
            P(("grp", "seq"), None),
            P(("grp", "seq")),
        ),
        out_specs=P(("grp", "seq"), None),
        check_vma=False,
    )
```

```python
import functools

import jax
import jax.numpy as jnp
from jax import lax
from jax.experimental import pallas as pl
from jax.experimental.pallas import tpu as pltpu
from jax.sharding import PartitionSpec as P

H = 32
KVH = 16
HD = 128
W = 1024


query_scale = 168.0 ** (-0.5)


def passed_along(value, axis, steps):
    count = lax.axis_size(axis)
    first, last = (max(0, -steps), min(count, count - steps))
    return lax.ppermute(value, axis, [(source, source + steps) for source in range(first, last)])


def rope_tables(doc_pos):
    half = HD // 2
    freqs = 10000.0 ** (-2.0 * jnp.arange(half, dtype=jnp.float32) / HD)
    angles = doc_pos.astype(jnp.float32)[:, None] * freqs[None, :]
    cos, sin = jnp.cos(angles), jnp.sin(angles)
    return jnp.concatenate([cos, cos], -1), jnp.concatenate([-sin, sin], -1)


def attend_kernel(par_ref, pos_ref, cos_ref, sin_ref, q_ref, k2a, k2b, k1, k0, v2a, v2b, v1, v0,
                  o_ref, *, rows, hops):
    span = (hops + 1) * rows
    cos = cos_ref[...]
    sin = sin_ref[...]

    def rot(x, c, s):
        return x * c + pltpu.roll(x, HD // 2, 1) * s

    even = par_ref[0] == 0
    k2 = jnp.where(even, k2a[...], k2b[...])
    v2 = jnp.where(even, v2a[...], v2b[...])
    k = jnp.concatenate([k2, k1[...], k0[...]], 0).astype(jnp.float32)
    k = rot(k, cos, sin).astype(jnp.bfloat16)
    v = jnp.concatenate([v2, v1[...], v0[...]], 0)
    qc = cos[span - rows:]
    qs = sin[span - rows:]
    dp = pos_ref[...]
    r = lax.broadcasted_iota(jnp.int32, (rows, span), 0)
    c = lax.broadcasted_iota(jnp.int32, (rows, span), 1)
    gap = (span - rows) + r - c
    vis = (gap >= 0) & (gap < W) & (gap <= dp)
    for g in range(2):
        q = q_ref[:, g * HD:(g + 1) * HD].astype(jnp.float32)
        q = rot(q, qc, qs).astype(jnp.bfloat16)
        s = lax.dot_general(q, k, (((1,), (1,)), ((), ())), preferred_element_type=jnp.float32)
        s = jnp.where(vis, s * query_scale, -1e30)
        m = jnp.max(s, axis=1, keepdims=True)
        w = jnp.where(vis, jnp.exp(s - m), 0.0)
        tot = jnp.sum(w, axis=1, keepdims=True)
        pv = jnp.dot(w.astype(jnp.bfloat16), v, preferred_element_type=jnp.float32)
        o_ref[:, g * HD:(g + 1) * HD] = (pv / tot).astype(jnp.bfloat16)


def local(queries, keys, values, segment_ids):
    rows = queries.shape[0]
    hops = W // rows
    assert hops == 2
    span = (hops + 1) * rows
    shard = lax.axis_index("seq")
    count = lax.axis_size("seq")
    seg_all = lax.all_gather(segment_ids, "seq", tiled=True)
    keys, values, seg_all = lax.optimization_barrier((keys, values, seg_all))
    near = lax.ppermute((keys, values), "seq", [(s, s + 1) for s in range(count - 1)])
    far = lax.ppermute((keys, values), "seq", [(s, s + 2) for s in range(0, count - 2, 2)])
    relay = lax.ppermute(near, "seq", [(s, s + 1) for s in range(0, count - 1, 2)])
    total = seg_all.shape[0]
    places = jnp.arange(total, dtype=jnp.int32)
    previous = jnp.concatenate([seg_all[:1], seg_all[:-1]])
    boundary = (seg_all != previous) | (places == 0)
    starts = lax.cummax(jnp.where(boundary, places, 0), axis=0)
    pos_all = jnp.concatenate([jnp.zeros((hops * rows,), jnp.int32), places - starts])
    pos_win = lax.dynamic_slice_in_dim(pos_all, shard * rows, span, 0)
    cos, sin = rope_tables(pos_win)
    pos_q = pos_win[span - rows:].reshape(rows, 1)
    parity = (shard % 2).astype(jnp.int32).reshape(1)
    kv_spec = pl.BlockSpec((rows, HD), lambda h, p: (0, h))
    full = lambda shape: pl.BlockSpec(shape, lambda h, p: (0, 0))
    kernel = functools.partial(attend_kernel, rows=rows, hops=hops)
    heads = keys.shape[1] // HD
    grid_spec = pltpu.PrefetchScalarGridSpec(
        num_scalar_prefetch=1,
        grid=(heads,),
        in_specs=[full((rows, 1)), full((span, HD)), full((span, HD)),
                  pl.BlockSpec((rows, 2 * HD), lambda h, p: (0, h))] + [kv_spec] * 8,
        out_specs=pl.BlockSpec((rows, 2 * HD), lambda h, p: (0, h)),
    )
    return pl.pallas_call(
        kernel,
        grid_spec=grid_spec,
        out_shape=jax.ShapeDtypeStruct(queries.shape, jnp.bfloat16),
        compiler_params=pltpu.CompilerParams(dimension_semantics=("arbitrary",)),
    )(parity, pos_q, cos, sin, queries, far[0], relay[0], near[0], keys,
      far[1], relay[1], near[1], values)


def solution(mesh):
    return jax.shard_map(
        local,
        mesh=mesh,
        in_specs=(
            P(("grp", "seq"), None),
            P(("grp", "seq"), None),
            P(("grp", "seq"), None),
            P(("grp", "seq")),
        ),
        out_specs=P(("grp", "seq"), None),
        check_vma=False,
    )
```

```python
import functools

import jax
import jax.numpy as jnp
from jax import lax
from jax.experimental import pallas as pl
from jax.experimental.pallas import tpu as pltpu
from jax.sharding import PartitionSpec as P

H = 32
KVH = 16
HD = 128
W = 1024


query_scale = 168.0 ** (-0.5)


def passed_along(value, axis, steps):
    count = lax.axis_size(axis)
    first, last = (max(0, -steps), min(count, count - steps))
    return lax.ppermute(value, axis, [(source, source + steps) for source in range(first, last)])


def rope_tables(doc_pos):
    half = HD // 2
    freqs = 10000.0 ** (-2.0 * jnp.arange(half, dtype=jnp.float32) / HD)
    angles = doc_pos.astype(jnp.float32)[:, None] * freqs[None, :]
    cos, sin = jnp.cos(angles), jnp.sin(angles)
    return jnp.concatenate([cos, cos], -1), jnp.concatenate([-sin, sin], -1)


def attend_kernel(par_ref, pos_ref, cos_ref, sin_ref, q_ref, k2a, k2b, k1, k0, v2a, v2b, v1, v0,
                  o_ref, bias_ref, *, rows, hops, tile):
    span = (hops + 1) * rows
    band = W + tile
    tiles = rows // tile

    @pl.when(pl.program_id(0) == 0)
    def _():
        dp = pos_ref[...]
        for a in range(tiles):
            r = lax.broadcasted_iota(jnp.int32, (tile, band), 0)
            c = lax.broadcasted_iota(jnp.int32, (tile, band), 1)
            gap = W + r - c
            vis = (gap >= 0) & (gap < W) & (gap <= dp[a * tile:(a + 1) * tile])
            bias_ref[a] = jnp.where(vis, 0.0, -1e30).astype(jnp.float32)

    cos = cos_ref[...]
    sin = sin_ref[...]

    def rot(x, c, s):
        return x * c + pltpu.roll(x, HD // 2, 1) * s

    even = par_ref[0] == 0
    k2 = jnp.where(even, k2a[...], k2b[...])
    v2 = jnp.where(even, v2a[...], v2b[...])
    k = jnp.concatenate([k2, k1[...], k0[...]], 0).astype(jnp.float32)
    k = rot(k, cos, sin).astype(jnp.bfloat16)
    v = jnp.concatenate([v2, v1[...], v0[...]], 0)
    off = span - rows
    for a in range(tiles):
        lo = a * tile
        kk = k[lo:lo + band]
        vv = v[lo:lo + band]
        bias = bias_ref[a]
        qc = cos[off + lo:off + lo + tile]
        qs = sin[off + lo:off + lo + tile]
        for g in range(2):
            q = q_ref[lo:lo + tile, g * HD:(g + 1) * HD].astype(jnp.float32)
            q = rot(q, qc, qs).astype(jnp.bfloat16)
            s = lax.dot_general(q, kk, (((1,), (1,)), ((), ())), preferred_element_type=jnp.float32)
            s = s * query_scale + bias
            m = jnp.max(s, axis=1, keepdims=True)
            w = jnp.exp(s - m)
            tot = jnp.sum(w, axis=1, keepdims=True)
            pv = jnp.dot(w.astype(jnp.bfloat16), vv, preferred_element_type=jnp.float32)
            o_ref[lo:lo + tile, g * HD:(g + 1) * HD] = (pv / tot).astype(jnp.bfloat16)


def local(queries, keys, values, segment_ids):
    rows = queries.shape[0]
    hops = W // rows
    assert hops == 2
    span = (hops + 1) * rows
    shard = lax.axis_index("seq")
    count = lax.axis_size("seq")
    seg_all = lax.all_gather(segment_ids, "seq", tiled=True)
    keys, values, seg_all = lax.optimization_barrier((keys, values, seg_all))
    near = lax.ppermute((keys, values), "seq", [(s, s + 1) for s in range(count - 1)])
    far = lax.ppermute((keys, values), "seq", [(s, s + 2) for s in range(0, count - 2, 2)])
    relay = lax.ppermute(near, "seq", [(s, s + 1) for s in range(0, count - 1, 2)])
    total = seg_all.shape[0]
    places = jnp.arange(total, dtype=jnp.int32)
    previous = jnp.concatenate([seg_all[:1], seg_all[:-1]])
    boundary = (seg_all != previous) | (places == 0)
    starts = lax.cummax(jnp.where(boundary, places, 0), axis=0)
    pos_all = jnp.concatenate([jnp.zeros((hops * rows,), jnp.int32), places - starts])
    pos_win = lax.dynamic_slice_in_dim(pos_all, shard * rows, span, 0)
    cos, sin = rope_tables(pos_win)
    pos_q = pos_win[span - rows:].reshape(rows, 1)
    parity = (shard % 2).astype(jnp.int32).reshape(1)
    kv_spec = pl.BlockSpec((rows, HD), lambda h, p: (0, h))
    full = lambda shape: pl.BlockSpec(shape, lambda h, p: (0, 0))
    tile = 128
    kernel = functools.partial(attend_kernel, rows=rows, hops=hops, tile=tile)
    heads = keys.shape[1] // HD
    grid_spec = pltpu.PrefetchScalarGridSpec(
        num_scalar_prefetch=1,
        grid=(heads,),
        in_specs=[full((rows, 1)), full((span, HD)), full((span, HD)),
                  pl.BlockSpec((rows, 2 * HD), lambda h, p: (0, h))] + [kv_spec] * 8,
        out_specs=pl.BlockSpec((rows, 2 * HD), lambda h, p: (0, h)),
        scratch_shapes=[pltpu.VMEM((rows // tile, tile, W + tile), jnp.float32)],
    )
    return pl.pallas_call(
        kernel,
        grid_spec=grid_spec,
        out_shape=jax.ShapeDtypeStruct(queries.shape, jnp.bfloat16),
        compiler_params=pltpu.CompilerParams(dimension_semantics=("arbitrary",)),
    )(parity, pos_q, cos, sin, queries, far[0], relay[0], near[0], keys,
      far[1], relay[1], near[1], values)


def solution(mesh):
    return jax.shard_map(
        local,
        mesh=mesh,
        in_specs=(
            P(("grp", "seq"), None),
            P(("grp", "seq"), None),
            P(("grp", "seq"), None),
            P(("grp", "seq")),
        ),
        out_specs=P(("grp", "seq"), None),
        check_vma=False,
    )
```

```python
import functools

import jax
import jax.numpy as jnp
from jax import lax
from jax.experimental import pallas as pl
from jax.experimental.pallas import tpu as pltpu
from jax.sharding import PartitionSpec as P

H = 32
KVH = 16
HD = 128
W = 1024


query_scale = 168.0 ** (-0.5)


def passed_along(value, axis, steps):
    count = lax.axis_size(axis)
    first, last = (max(0, -steps), min(count, count - steps))
    return lax.ppermute(value, axis, [(source, source + steps) for source in range(first, last)])


def rope_tables(doc_pos):
    half = HD // 2
    freqs = 10000.0 ** (-2.0 * jnp.arange(half, dtype=jnp.float32) / HD)
    angles = doc_pos.astype(jnp.float32)[:, None] * freqs[None, :]
    cos, sin = jnp.cos(angles), jnp.sin(angles)
    return jnp.concatenate([cos, cos], -1), jnp.concatenate([-sin, sin], -1)


def attend_kernel(par_ref, pos_ref, cos_ref, sin_ref, q_ref, *refs, rows, tile, first, final):
    if final:
        k2a, k2b, v2a, v2b, m_in, l_in, acc_in, o_ref, bias_ref = refs
    else:
        k1, k0, v1, v0, m_out, l_out, acc_out, bias_ref = refs
    tiles = rows // tile
    nkeys = bias_ref.shape[2]
    qoff = W

    def bounds(a):
        lo = max(0, a * tile - first)
        hi = min(nkeys, a * tile + W + tile - first)
        return lo, hi

    @pl.when(pl.program_id(0) == 0)
    def _():
        dp = pos_ref[...]
        for a in range(tiles):
            r = lax.broadcasted_iota(jnp.int32, (tile, nkeys), 0) + a * tile
            c = lax.broadcasted_iota(jnp.int32, (tile, nkeys), 1) + first
            gap = qoff + r - c
            vis = (gap >= 0) & (gap < W) & (gap <= dp[a * tile:(a + 1) * tile])
            bias_ref[a] = jnp.where(vis, 0.0, -1e30).astype(jnp.float32)

    cos = cos_ref[...]
    sin = sin_ref[...]

    def rot(x, c, s):
        return x * c + pltpu.roll(x, HD // 2, 1) * s

    if final:
        even = par_ref[0] == 0
        k = jnp.where(even, k2a[...], k2b[...])
        v = jnp.where(even, v2a[...], v2b[...])
    else:
        k = jnp.concatenate([k1[...], k0[...]], 0)
        v = jnp.concatenate([v1[...], v0[...]], 0)
    k = rot(k.astype(jnp.float32), cos[first:first + nkeys], sin[first:first + nkeys])
    k = k.astype(jnp.bfloat16)
    for a in range(tiles):
        lo, hi = bounds(a)
        r0 = a * tile
        kk = k[lo:hi]
        vv = v[lo:hi]
        bias = bias_ref[a, :, lo:hi]
        qc = cos[qoff + r0:qoff + r0 + tile]
        qs = sin[qoff + r0:qoff + r0 + tile]
        for g in range(2):
            cols = slice(g * HD, (g + 1) * HD)
            q = q_ref[r0:r0 + tile, cols].astype(jnp.float32)
            q = rot(q, qc, qs).astype(jnp.bfloat16)
            s = lax.dot_general(q, kk, (((1,), (1,)), ((), ())), preferred_element_type=jnp.float32)
            s = s * query_scale + bias
            m = jnp.max(s, axis=1, keepdims=True)
            if final:
                m1 = m_in[g, r0:r0 + tile]
                mm = jnp.maximum(m, m1)
                scale1 = jnp.exp(m1 - mm)
                w = jnp.exp(s - mm)
                tot = jnp.sum(w, axis=1, keepdims=True) + l_in[g, r0:r0 + tile] * scale1
                pv = jnp.dot(w.astype(jnp.bfloat16), vv, preferred_element_type=jnp.float32)
                pv = pv + acc_in[r0:r0 + tile, cols] * scale1
                o_ref[r0:r0 + tile, cols] = (pv / tot).astype(jnp.bfloat16)
            else:
                w = jnp.exp(s - m)
                m_out[g, r0:r0 + tile] = m
                l_out[g, r0:r0 + tile] = jnp.sum(w, axis=1, keepdims=True)
                acc_out[r0:r0 + tile, cols] = jnp.dot(
                    w.astype(jnp.bfloat16), vv, preferred_element_type=jnp.float32)


def local(queries, keys, values, segment_ids):
    rows = queries.shape[0]
    hops = W // rows
    assert hops == 2
    span = (hops + 1) * rows
    shard = lax.axis_index("seq")
    count = lax.axis_size("seq")
    seg_all = lax.all_gather(segment_ids, "seq", tiled=True)
    keys, values, seg_all = lax.optimization_barrier((keys, values, seg_all))
    near = lax.ppermute((keys, values), "seq", [(s, s + 1) for s in range(count - 1)])
    keys_b, values_b, near = lax.optimization_barrier((keys, values, near))
    far = lax.ppermute((keys_b, values_b), "seq", [(s, s + 2) for s in range(0, count - 2, 2)])
    relay = lax.ppermute(near, "seq", [(s, s + 1) for s in range(0, count - 1, 2)])
    total = seg_all.shape[0]
    places = jnp.arange(total, dtype=jnp.int32)
    previous = jnp.concatenate([seg_all[:1], seg_all[:-1]])
    boundary = (seg_all != previous) | (places == 0)
    starts = lax.cummax(jnp.where(boundary, places, 0), axis=0)
    pos_all = jnp.concatenate([jnp.zeros((hops * rows,), jnp.int32), places - starts])
    pos_win = lax.dynamic_slice_in_dim(pos_all, shard * rows, span, 0)
    cos, sin = rope_tables(pos_win)
    pos_q = pos_win[span - rows:].reshape(rows, 1)
    parity = (shard % 2).astype(jnp.int32).reshape(1)
    tile = 128
    heads = keys.shape[1] // HD
    kv_spec = pl.BlockSpec((rows, HD), lambda h, p: (0, h))
    full = lambda shape: pl.BlockSpec(shape, lambda h, p: (0, 0))
    head_spec = pl.BlockSpec((rows, 2 * HD), lambda h, p: (0, h))
    stat_spec = pl.BlockSpec((2, rows, 1), lambda h, p: (h, 0, 0))
    lead = [full((rows, 1)), full((span, HD)), full((span, HD)), head_spec]
    params = pltpu.CompilerParams(dimension_semantics=("arbitrary",))
    f32 = jnp.float32
    stat_shape = jax.ShapeDtypeStruct((2 * heads, rows, 1), f32)
    m1, l1, acc1 = pl.pallas_call(
        functools.partial(attend_kernel, rows=rows, tile=tile, first=rows, final=False),
        grid_spec=pltpu.PrefetchScalarGridSpec(
            num_scalar_prefetch=1, grid=(heads,),
            in_specs=lead + [kv_spec] * 4,
            out_specs=[stat_spec, stat_spec, head_spec],
            scratch_shapes=[pltpu.VMEM((rows // tile, tile, 2 * rows), f32)]),
        out_shape=[stat_shape, stat_shape, jax.ShapeDtypeStruct(queries.shape, f32)],
        compiler_params=params,
    )(parity, pos_q, cos, sin, queries, near[0], keys, near[1], values)
    return pl.pallas_call(
        functools.partial(attend_kernel, rows=rows, tile=tile, first=0, final=True),
        grid_spec=pltpu.PrefetchScalarGridSpec(
            num_scalar_prefetch=1, grid=(heads,),
            in_specs=lead + [kv_spec] * 4 + [stat_spec, stat_spec, head_spec],
            out_specs=head_spec,
            scratch_shapes=[pltpu.VMEM((rows // tile, tile, rows), f32)]),
        out_shape=jax.ShapeDtypeStruct(queries.shape, jnp.bfloat16),
        compiler_params=params,
    )(parity, pos_q, cos, sin, queries, far[0], relay[0], far[1], relay[1], m1, l1, acc1)


def solution(mesh):
    return jax.shard_map(
        local,
        mesh=mesh,
        in_specs=(
            P(("grp", "seq"), None),
            P(("grp", "seq"), None),
            P(("grp", "seq"), None),
            P(("grp", "seq")),
        ),
        out_specs=P(("grp", "seq"), None),
        check_vma=False,
    )
```

```python
import functools

import jax
import jax.numpy as jnp
from jax import lax
from jax.experimental import pallas as pl
from jax.experimental.pallas import tpu as pltpu
from jax.sharding import PartitionSpec as P

H = 32
KVH = 16
HD = 128
W = 1024


query_scale = 168.0 ** (-0.5)
exp2_scale = query_scale * 1.4426950408889634


def passed_along(value, axis, steps):
    count = lax.axis_size(axis)
    first, last = (max(0, -steps), min(count, count - steps))
    return lax.ppermute(value, axis, [(source, source + steps) for source in range(first, last)])


def rope_tables(doc_pos):
    half = HD // 2
    freqs = 10000.0 ** (-2.0 * jnp.arange(half, dtype=jnp.float32) / HD)
    angles = doc_pos.astype(jnp.float32)[:, None] * freqs[None, :]
    cos, sin = jnp.cos(angles), jnp.sin(angles)
    return jnp.concatenate([cos, cos], -1), jnp.concatenate([-sin, sin], -1)


def attend_kernel(par_ref, pos_ref, cos_ref, sin_ref, q_ref, k2a, k2b, k1, k0, v2a, v2b, v1, v0,
                  o_ref, bias_ref, *, rows, hops, tile):
    span = (hops + 1) * rows
    band = W + tile
    tiles = rows // tile

    @pl.when(pl.program_id(0) == 0)
    def _():
        dp = pos_ref[...]
        for a in range(tiles):
            r = lax.broadcasted_iota(jnp.int32, (tile, band), 0)
            c = lax.broadcasted_iota(jnp.int32, (tile, band), 1)
            gap = W + r - c
            vis = (gap >= 0) & (gap < W) & (gap <= dp[a * tile:(a + 1) * tile])
            bias_ref[a] = jnp.where(vis, 0.0, -1e30).astype(jnp.float32)

    cos = cos_ref[...]
    sin = sin_ref[...]

    def rot(x, c, s):
        return x * c + pltpu.roll(x, HD // 2, 1) * s

    even = par_ref[0] == 0
    k2 = jnp.where(even, k2a[...], k2b[...])
    v2 = jnp.where(even, v2a[...], v2b[...])
    k = jnp.concatenate([k2, k1[...], k0[...]], 0).astype(jnp.float32)
    k = rot(k, cos, sin).astype(jnp.bfloat16)
    v = jnp.concatenate([v2, v1[...], v0[...]], 0)
    off = span - rows
    for a in range(tiles):
        lo = a * tile
        kk = k[lo:lo + band]
        vv = v[lo:lo + band]
        bias = bias_ref[a]
        qc = cos[off + lo:off + lo + tile]
        qs = sin[off + lo:off + lo + tile]
        for g in range(2):
            q = q_ref[lo:lo + tile, g * HD:(g + 1) * HD].astype(jnp.float32)
            q = rot(q, qc, qs).astype(jnp.bfloat16)
            s = lax.dot_general(q, kk, (((1,), (1,)), ((), ())), preferred_element_type=jnp.float32)
            s = s + bias
            m = jnp.max(s, axis=1, keepdims=True)
            w = jnp.exp2((s - m) * exp2_scale)
            tot = jnp.sum(w, axis=1, keepdims=True)
            pv = jnp.dot(w.astype(jnp.bfloat16), vv, preferred_element_type=jnp.float32)
            o_ref[lo:lo + tile, g * HD:(g + 1) * HD] = (pv / tot).astype(jnp.bfloat16)


def local(queries, keys, values, segment_ids):
    rows = queries.shape[0]
    hops = W // rows
    assert hops == 2
    span = (hops + 1) * rows
    shard = lax.axis_index("seq")
    count = lax.axis_size("seq")
    near = lax.ppermute((keys, values), "seq", [(s, s + 1) for s in range(count - 1)])
    seg_all = lax.all_gather(segment_ids, "seq", tiled=True)
    keys, values, seg_all = lax.optimization_barrier((keys, values, seg_all))
    far = lax.ppermute((keys, values), "seq", [(s, s + 2) for s in range(0, count - 2, 2)])
    relay = lax.ppermute(near, "seq", [(s, s + 1) for s in range(0, count - 1, 2)])
    total = seg_all.shape[0]
    places = jnp.arange(total, dtype=jnp.int32)
    previous = jnp.concatenate([seg_all[:1], seg_all[:-1]])
    boundary = (seg_all != previous) | (places == 0)
    starts = lax.cummax(jnp.where(boundary, places, 0), axis=0)
    pos_all = jnp.concatenate([jnp.zeros((hops * rows,), jnp.int32), places - starts])
    pos_win = lax.dynamic_slice_in_dim(pos_all, shard * rows, span, 0)
    cos, sin = rope_tables(pos_win)
    pos_q = pos_win[span - rows:].reshape(rows, 1)
    parity = (shard % 2).astype(jnp.int32).reshape(1)
    kv_spec = pl.BlockSpec((rows, HD), lambda h, p: (0, h))
    full = lambda shape: pl.BlockSpec(shape, lambda h, p: (0, 0))
    tile = 128
    kernel = functools.partial(attend_kernel, rows=rows, hops=hops, tile=tile)
    heads = keys.shape[1] // HD
    grid_spec = pltpu.PrefetchScalarGridSpec(
        num_scalar_prefetch=1,
        grid=(heads,),
        in_specs=[full((rows, 1)), full((span, HD)), full((span, HD)),
                  pl.BlockSpec((rows, 2 * HD), lambda h, p: (0, h))] + [kv_spec] * 8,
        out_specs=pl.BlockSpec((rows, 2 * HD), lambda h, p: (0, h)),
        scratch_shapes=[pltpu.VMEM((rows // tile, tile, W + tile), jnp.float32)],
    )
    return pl.pallas_call(
        kernel,
        grid_spec=grid_spec,
        out_shape=jax.ShapeDtypeStruct(queries.shape, jnp.bfloat16),
        compiler_params=pltpu.CompilerParams(dimension_semantics=("arbitrary",)),
    )(parity, pos_q, cos, sin, queries, far[0], relay[0], near[0], keys,
      far[1], relay[1], near[1], values)


def solution(mesh):
    return jax.shard_map(
        local,
        mesh=mesh,
        in_specs=(
            P(("grp", "seq"), None),
            P(("grp", "seq"), None),
            P(("grp", "seq"), None),
            P(("grp", "seq")),
        ),
        out_specs=P(("grp", "seq"), None),
        check_vma=False,
    )
```

```python
import functools

import jax
import jax.numpy as jnp
from jax import lax
from jax.experimental import pallas as pl
from jax.experimental.pallas import tpu as pltpu
from jax.sharding import PartitionSpec as P

H = 32
KVH = 16
HD = 128
W = 1024


query_scale = 168.0 ** (-0.5)
exp2_scale = query_scale * 1.4426950408889634


def passed_along(value, axis, steps):
    count = lax.axis_size(axis)
    first, last = (max(0, -steps), min(count, count - steps))
    return lax.ppermute(value, axis, [(source, source + steps) for source in range(first, last)])


def rope_tables(doc_pos):
    half = HD // 2
    freqs = 10000.0 ** (-2.0 * jnp.arange(half, dtype=jnp.float32) / HD)
    angles = doc_pos.astype(jnp.float32)[:, None] * freqs[None, :]
    cos, sin = jnp.cos(angles), jnp.sin(angles)
    return jnp.concatenate([cos, cos], -1), jnp.concatenate([-sin, sin], -1)


def attend_kernel(par_ref, pos_ref, cos_ref, sin_ref, q_ref, k2a, k2b, k1, k0, v2a, v2b, v1, v0,
                  o_ref, bias_ref, *, rows, hops, tile):
    span = (hops + 1) * rows
    band = W + tile
    tiles = rows // tile

    @pl.when(pl.program_id(0) == 0)
    def _():
        dp = pos_ref[...]
        for a in range(tiles):
            r = lax.broadcasted_iota(jnp.int32, (tile, band), 0)
            c = lax.broadcasted_iota(jnp.int32, (tile, band), 1)
            gap = W + r - c
            vis = (gap >= 0) & (gap < W) & (gap <= dp[a * tile:(a + 1) * tile])
            bias_ref[a] = jnp.where(vis, 0.0, -1e30).astype(jnp.float32)

    cos = cos_ref[...]
    sin = sin_ref[...]

    def rot(x, c, s):
        return x * c + pltpu.roll(x, HD // 2, 1) * s

    even = par_ref[0] == 0
    k2 = jnp.where(even, k2a[...], k2b[...])
    v2 = jnp.where(even, v2a[...], v2b[...])
    k = jnp.concatenate([k2, k1[...], k0[...]], 0).astype(jnp.float32)
    k = rot(k, cos, sin).astype(jnp.bfloat16)
    v = jnp.concatenate([v2, v1[...], v0[...]], 0)
    off = span - rows
    for a in range(tiles):
        lo = a * tile
        kk = k[lo:lo + band]
        vv = v[lo:lo + band]
        bias = bias_ref[a]
        qc = cos[off + lo:off + lo + tile]
        qs = sin[off + lo:off + lo + tile]
        for g in range(2):
            q = q_ref[lo:lo + tile, g * HD:(g + 1) * HD].astype(jnp.float32)
            q = rot(q, qc, qs).astype(jnp.bfloat16)
            s = lax.dot_general(q, kk, (((1,), (1,)), ((), ())), preferred_element_type=jnp.float32)
            s = s + bias
            m = jnp.max(s, axis=1, keepdims=True)
            w = jnp.exp2((s - m) * exp2_scale)
            tot = jnp.sum(w, axis=1, keepdims=True)
            pv = jnp.dot(w.astype(jnp.bfloat16), vv, preferred_element_type=jnp.float32)
            o_ref[lo:lo + tile, g * HD:(g + 1) * HD] = (pv / tot).astype(jnp.bfloat16)


def local(queries, keys, values, segment_ids):
    rows = queries.shape[0]
    hops = W // rows
    assert hops == 2
    span = (hops + 1) * rows
    shard = lax.axis_index("seq")
    count = lax.axis_size("seq")
    near = lax.ppermute((keys, values), "seq", [(s, s + 1) for s in range(count - 1)])
    far = lax.ppermute((keys, values), "seq", [(s, s + 2) for s in range(0, count - 2, 2)])
    relay = lax.ppermute(near, "seq", [(s, s + 1) for s in range(0, count - 1, 2)])
    segment_ids, near = lax.optimization_barrier((segment_ids, near))
    seg_all = lax.all_gather(segment_ids, "seq", tiled=True)
    total = seg_all.shape[0]
    places = jnp.arange(total, dtype=jnp.int32)
    previous = jnp.concatenate([seg_all[:1], seg_all[:-1]])
    boundary = (seg_all != previous) | (places == 0)
    starts = lax.cummax(jnp.where(boundary, places, 0), axis=0)
    pos_all = jnp.concatenate([jnp.zeros((hops * rows,), jnp.int32), places - starts])
    pos_win = lax.dynamic_slice_in_dim(pos_all, shard * rows, span, 0)
    cos, sin = rope_tables(pos_win)
    pos_q = pos_win[span - rows:].reshape(rows, 1)
    parity = (shard % 2).astype(jnp.int32).reshape(1)
    kv_spec = pl.BlockSpec((rows, HD), lambda h, p: (0, h))
    full = lambda shape: pl.BlockSpec(shape, lambda h, p: (0, 0))
    tile = 128
    kernel = functools.partial(attend_kernel, rows=rows, hops=hops, tile=tile)
    heads = keys.shape[1] // HD
    grid_spec = pltpu.PrefetchScalarGridSpec(
        num_scalar_prefetch=1,
        grid=(heads,),
        in_specs=[full((rows, 1)), full((span, HD)), full((span, HD)),
                  pl.BlockSpec((rows, 2 * HD), lambda h, p: (0, h))] + [kv_spec] * 8,
        out_specs=pl.BlockSpec((rows, 2 * HD), lambda h, p: (0, h)),
        scratch_shapes=[pltpu.VMEM((rows // tile, tile, W + tile), jnp.float32)],
    )
    return pl.pallas_call(
        kernel,
        grid_spec=grid_spec,
        out_shape=jax.ShapeDtypeStruct(queries.shape, jnp.bfloat16),
        compiler_params=pltpu.CompilerParams(dimension_semantics=("arbitrary",)),
    )(parity, pos_q, cos, sin, queries, far[0], relay[0], near[0], keys,
      far[1], relay[1], near[1], values)


def solution(mesh):
    return jax.shard_map(
        local,
        mesh=mesh,
        in_specs=(
            P(("grp", "seq"), None),
            P(("grp", "seq"), None),
            P(("grp", "seq"), None),
            P(("grp", "seq")),
        ),
        out_specs=P(("grp", "seq"), None),
        check_vma=False,
    )
```

```python
import functools

import jax
import jax.numpy as jnp
from jax import lax
from jax.experimental import pallas as pl
from jax.experimental.pallas import tpu as pltpu
from jax.sharding import PartitionSpec as P

H = 32
KVH = 16
HD = 128
W = 1024


query_scale = 168.0 ** (-0.5)
exp2_scale = query_scale * 1.4426950408889634


def passed_along(value, axis, steps):
    count = lax.axis_size(axis)
    first, last = (max(0, -steps), min(count, count - steps))
    return lax.ppermute(value, axis, [(source, source + steps) for source in range(first, last)])


def rope_tables(doc_pos):
    half = HD // 2
    freqs = 10000.0 ** (-2.0 * jnp.arange(half, dtype=jnp.float32) / HD)
    angles = doc_pos.astype(jnp.float32)[:, None] * freqs[None, :]
    cos, sin = jnp.cos(angles), jnp.sin(angles)
    return jnp.concatenate([cos, cos], -1), jnp.concatenate([-sin, sin], -1)


def attend_kernel(par_ref, pos_ref, cos_ref, sin_ref, q_ref, *refs, rows, tile, first, final):
    if final:
        k2a, k2b, v2a, v2b, st_in, acc_in, o_ref, bias_ref = refs
    else:
        k1, k0, v1, v0, st_out, acc_out, bias_ref = refs
    tiles = rows // tile
    nkeys = bias_ref.shape[2]
    qoff = W

    def bounds(a):
        lo = max(0, a * tile - first)
        hi = min(nkeys, a * tile + W + tile - first)
        return lo, hi

    @pl.when(pl.program_id(0) == 0)
    def _():
        dp = pos_ref[...]
        for a in range(tiles):
            r = lax.broadcasted_iota(jnp.int32, (tile, nkeys), 0) + a * tile
            c = lax.broadcasted_iota(jnp.int32, (tile, nkeys), 1) + first
            gap = qoff + r - c
            vis = (gap >= 0) & (gap < W) & (gap <= dp[a * tile:(a + 1) * tile])
            bias_ref[a] = jnp.where(vis, 0.0, -1e30).astype(jnp.float32)

    cos = cos_ref[...]
    sin = sin_ref[...]

    def rot(x, c, s):
        return x * c + pltpu.roll(x, HD // 2, 1) * s

    if final:
        even = par_ref[0] == 0
        k = jnp.where(even, k2a[...], k2b[...])
        v = jnp.where(even, v2a[...], v2b[...])
    else:
        k = jnp.concatenate([k1[...], k0[...]], 0)
        v = jnp.concatenate([v1[...], v0[...]], 0)
    k = rot(k.astype(jnp.float32), cos[first:first + nkeys], sin[first:first + nkeys])
    k = k.astype(jnp.bfloat16)
    for a in range(tiles):
        lo, hi = bounds(a)
        r0 = a * tile
        kk = k[lo:hi]
        vv = v[lo:hi]
        bias = bias_ref[a, :, lo:hi]
        qc = cos[qoff + r0:qoff + r0 + tile]
        qs = sin[qoff + r0:qoff + r0 + tile]
        for g in range(2):
            cols = slice(g * HD, (g + 1) * HD)
            q = q_ref[r0:r0 + tile, cols].astype(jnp.float32)
            q = rot(q, qc, qs).astype(jnp.bfloat16)
            s = lax.dot_general(q, kk, (((1,), (1,)), ((), ())), preferred_element_type=jnp.float32)
            s = s + bias
            m = jnp.max(s, axis=1, keepdims=True)
            if final:
                m1 = st_in[0, r0:r0 + tile, g:g + 1]
                mm = jnp.maximum(m, m1)
                scale1 = jnp.exp2((m1 - mm) * exp2_scale)
                w = jnp.exp2((s - mm) * exp2_scale)
                tot = jnp.sum(w, axis=1, keepdims=True) + st_in[0, r0:r0 + tile, 2 + g:3 + g] * scale1
                pv = jnp.dot(w.astype(jnp.bfloat16), vv, preferred_element_type=jnp.float32)
                pv = pv + acc_in[r0:r0 + tile, cols] * scale1
                o_ref[r0:r0 + tile, cols] = (pv / tot).astype(jnp.bfloat16)
            else:
                w = jnp.exp2((s - m) * exp2_scale)
                st_out[0, r0:r0 + tile, g:g + 1] = m
                st_out[0, r0:r0 + tile, 2 + g:3 + g] = jnp.sum(w, axis=1, keepdims=True)
                acc_out[r0:r0 + tile, cols] = jnp.dot(
                    w.astype(jnp.bfloat16), vv, preferred_element_type=jnp.float32)


def local(queries, keys, values, segment_ids):
    rows = queries.shape[0]
    hops = W // rows
    assert hops == 2
    span = (hops + 1) * rows
    shard = lax.axis_index("seq")
    count = lax.axis_size("seq")
    near = lax.ppermute((keys, values), "seq", [(s, s + 1) for s in range(count - 1)])
    seg_all = lax.all_gather(segment_ids, "seq", tiled=True)
    keys_b, values_b, seg_all = lax.optimization_barrier((keys, values, seg_all))
    far = lax.ppermute((keys_b, values_b), "seq", [(s, s + 2) for s in range(0, count - 2, 2)])
    relay = lax.ppermute(near, "seq", [(s, s + 1) for s in range(0, count - 1, 2)])
    total = seg_all.shape[0]
    places = jnp.arange(total, dtype=jnp.int32)
    previous = jnp.concatenate([seg_all[:1], seg_all[:-1]])
    boundary = (seg_all != previous) | (places == 0)
    starts = lax.cummax(jnp.where(boundary, places, 0), axis=0)
    pos_all = jnp.concatenate([jnp.zeros((hops * rows,), jnp.int32), places - starts])
    pos_win = lax.dynamic_slice_in_dim(pos_all, shard * rows, span, 0)
    cos, sin = rope_tables(pos_win)
    pos_q = pos_win[span - rows:].reshape(rows, 1)
    parity = (shard % 2).astype(jnp.int32).reshape(1)
    tile = 128
    heads = keys.shape[1] // HD
    kv_spec = pl.BlockSpec((rows, HD), lambda h, p: (0, h))
    full = lambda shape: pl.BlockSpec(shape, lambda h, p: (0, 0))
    head_spec = pl.BlockSpec((rows, 2 * HD), lambda h, p: (0, h))
    stat_spec = pl.BlockSpec((1, rows, 128), lambda h, p: (h, 0, 0))
    lead = [full((rows, 1)), full((span, HD)), full((span, HD)), head_spec]
    params = pltpu.CompilerParams(dimension_semantics=("arbitrary",))
    f32 = jnp.float32
    stats, acc1 = pl.pallas_call(
        functools.partial(attend_kernel, rows=rows, tile=tile, first=rows, final=False),
        grid_spec=pltpu.PrefetchScalarGridSpec(
            num_scalar_prefetch=1, grid=(heads,),
            in_specs=lead + [kv_spec] * 4,
            out_specs=[stat_spec, head_spec],
            scratch_shapes=[pltpu.VMEM((rows // tile, tile, 2 * rows), f32)]),
        out_shape=[jax.ShapeDtypeStruct((heads, rows, 128), f32),
                   jax.ShapeDtypeStruct(queries.shape, f32)],
        compiler_params=params,
    )(parity, pos_q, cos, sin, queries, near[0], keys, near[1], values)
    return pl.pallas_call(
        functools.partial(attend_kernel, rows=rows, tile=tile, first=0, final=True),
        grid_spec=pltpu.PrefetchScalarGridSpec(
            num_scalar_prefetch=1, grid=(heads,),
            in_specs=lead + [kv_spec] * 4 + [stat_spec, head_spec],
            out_specs=head_spec,
            scratch_shapes=[pltpu.VMEM((rows // tile, tile, rows), f32)]),
        out_shape=jax.ShapeDtypeStruct(queries.shape, jnp.bfloat16),
        compiler_params=params,
    )(parity, pos_q, cos, sin, queries, far[0], relay[0], far[1], relay[1], stats, acc1)


def solution(mesh):
    return jax.shard_map(
        local,
        mesh=mesh,
        in_specs=(
            P(("grp", "seq"), None),
            P(("grp", "seq"), None),
            P(("grp", "seq"), None),
            P(("grp", "seq")),
        ),
        out_specs=P(("grp", "seq"), None),
        check_vma=False,
    )
```

```python
import functools

import jax
import jax.numpy as jnp
from jax import lax
from jax.experimental import pallas as pl
from jax.experimental.pallas import tpu as pltpu
from jax.sharding import PartitionSpec as P

H = 32
KVH = 16
HD = 128
W = 1024


query_scale = 168.0 ** (-0.5)
exp2_scale = query_scale * 1.4426950408889634


def passed_along(value, axis, steps):
    count = lax.axis_size(axis)
    first, last = (max(0, -steps), min(count, count - steps))
    return lax.ppermute(value, axis, [(source, source + steps) for source in range(first, last)])


def rope_tables(doc_pos):
    half = HD // 2
    freqs = 10000.0 ** (-2.0 * jnp.arange(half, dtype=jnp.float32) / HD)
    angles = doc_pos.astype(jnp.float32)[:, None] * freqs[None, :]
    cos, sin = jnp.cos(angles), jnp.sin(angles)
    return jnp.concatenate([cos, cos], -1), jnp.concatenate([-sin, sin], -1)


def attend_kernel(par_ref, pos_ref, cos_ref, sin_ref, q_ref, k2a, k2b, k1, k0, v2a, v2b, v1, v0,
                  o_ref, bias_ref, *, rows, hops, tile):
    span = (hops + 1) * rows
    band = W + tile
    tiles = rows // tile

    @pl.when(pl.program_id(0) == 0)
    def _():
        dp = pos_ref[...]
        for a in range(tiles):
            r = lax.broadcasted_iota(jnp.int32, (tile, band), 0)
            c = lax.broadcasted_iota(jnp.int32, (tile, band), 1)
            gap = W + r - c
            vis = (gap >= 0) & (gap < W) & (gap <= dp[a * tile:(a + 1) * tile])
            bias_ref[a] = jnp.where(vis, 0.0, -1e30).astype(jnp.float32)

    cos = cos_ref[...]
    sin = sin_ref[...]

    def rot(x, c, s):
        return x * c + pltpu.roll(x, HD // 2, 1) * s

    even = par_ref[0] == 0
    k2 = jnp.where(even, k2a[...], k2b[...])
    v2 = jnp.where(even, v2a[...], v2b[...])
    k = jnp.concatenate([k2, k1[...], k0[...]], 0).astype(jnp.float32)
    k = rot(k, cos, sin).astype(jnp.bfloat16)
    v = jnp.concatenate([v2, v1[...], v0[...]], 0)
    off = span - rows
    for a in range(tiles):
        lo = a * tile
        kk = k[lo:lo + band]
        vv = v[lo:lo + band]
        bias = bias_ref[a]
        qc = cos[off + lo:off + lo + tile]
        qs = sin[off + lo:off + lo + tile]
        for g in range(2):
            q = q_ref[lo:lo + tile, g * HD:(g + 1) * HD].astype(jnp.float32)
            q = rot(q, qc, qs).astype(jnp.bfloat16)
            s = lax.dot_general(q, kk, (((1,), (1,)), ((), ())), preferred_element_type=jnp.float32)
            s = s + bias
            m = jnp.max(s, axis=1, keepdims=True)
            w = jnp.exp2((s - m) * exp2_scale)
            tot = jnp.sum(w, axis=1, keepdims=True)
            pv = jnp.dot(w.astype(jnp.bfloat16), vv, preferred_element_type=jnp.float32)
            o_ref[lo:lo + tile, g * HD:(g + 1) * HD] = (pv / tot).astype(jnp.bfloat16)


def local(queries, keys, values, segment_ids):
    rows = queries.shape[0]
    hops = W // rows
    assert hops == 2
    span = (hops + 1) * rows
    shard = lax.axis_index("seq")
    count = lax.axis_size("seq")
    near = lax.ppermute((keys, values), "seq", [(s, s + 1) for s in range(count - 1)])
    seg_all = lax.all_gather(segment_ids, "seq", tiled=True)
    keys, values, seg_all = lax.optimization_barrier((keys, values, seg_all))
    far = lax.ppermute((keys, values), "seq", [(s, s + 2) for s in range(0, count - 2, 2)])
    relay = lax.ppermute(near, "seq", [(s, s + 1) for s in range(0, count - 1, 2)])
    total = seg_all.shape[0]
    places = jnp.arange(total, dtype=jnp.int32)
    previous = jnp.concatenate([seg_all[:1], seg_all[:-1]])
    boundary = (seg_all != previous) | (places == 0)
    starts = lax.cummax(jnp.where(boundary, places, 0), axis=0)
    pos_all = jnp.concatenate([jnp.zeros((hops * rows,), jnp.int32), places - starts])
    pos_win = lax.dynamic_slice_in_dim(pos_all, shard * rows, span, 0)
    cos, sin = rope_tables(pos_win)
    pos_q = pos_win[span - rows:].reshape(rows, 1)
    parity = (shard % 2).astype(jnp.int32).reshape(1)
    kv_spec = pl.BlockSpec((rows, HD), lambda h, p: (0, h))
    full = lambda shape: pl.BlockSpec(shape, lambda h, p: (0, 0))
    tile = 256
    kernel = functools.partial(attend_kernel, rows=rows, hops=hops, tile=tile)
    heads = keys.shape[1] // HD
    grid_spec = pltpu.PrefetchScalarGridSpec(
        num_scalar_prefetch=1,
        grid=(heads,),
        in_specs=[full((rows, 1)), full((span, HD)), full((span, HD)),
                  pl.BlockSpec((rows, 2 * HD), lambda h, p: (0, h))] + [kv_spec] * 8,
        out_specs=pl.BlockSpec((rows, 2 * HD), lambda h, p: (0, h)),
        scratch_shapes=[pltpu.VMEM((rows // tile, tile, W + tile), jnp.float32)],
    )
    return pl.pallas_call(
        kernel,
        grid_spec=grid_spec,
        out_shape=jax.ShapeDtypeStruct(queries.shape, jnp.bfloat16),
        compiler_params=pltpu.CompilerParams(dimension_semantics=("arbitrary",)),
    )(parity, pos_q, cos, sin, queries, far[0], relay[0], near[0], keys,
      far[1], relay[1], near[1], values)


def solution(mesh):
    return jax.shard_map(
        local,
        mesh=mesh,
        in_specs=(
            P(("grp", "seq"), None),
            P(("grp", "seq"), None),
            P(("grp", "seq"), None),
            P(("grp", "seq")),
        ),
        out_specs=P(("grp", "seq"), None),
        check_vma=False,
    )
```

```python
import functools

import jax
import jax.numpy as jnp
from jax import lax
from jax.experimental import pallas as pl
from jax.experimental.pallas import tpu as pltpu
from jax.sharding import PartitionSpec as P


HD = 128
W = 1024


query_scale = 168.0 ** (-0.5)
exp2_scale = query_scale * 1.4426950408889634


def rope_tables(doc_pos):
    half = HD // 2
    freqs = 10000.0 ** (-2.0 * jnp.arange(half, dtype=jnp.float32) / HD)
    angles = doc_pos.astype(jnp.float32)[:, None] * freqs[None, :]
    cos, sin = jnp.cos(angles), jnp.sin(angles)
    return jnp.concatenate([cos, cos], -1), jnp.concatenate([-sin, sin], -1)


def attend_kernel(par_ref, pos_ref, cos_ref, sin_ref, q_ref, k2a, k2b, k1, k0, v2a, v2b, v1, v0,
                  o_ref, bias_ref, *, rows, hops, tile):
    span = (hops + 1) * rows
    band = W + tile
    tiles = rows // tile

    @pl.when(pl.program_id(0) == 0)
    def _():
        dp = pos_ref[...]
        for a in range(tiles):
            r = lax.broadcasted_iota(jnp.int32, (tile, band), 0)
            c = lax.broadcasted_iota(jnp.int32, (tile, band), 1)
            gap = W + r - c
            vis = (gap >= 0) & (gap < W) & (gap <= dp[a * tile:(a + 1) * tile])
            bias_ref[a] = jnp.where(vis, 0.0, -1e30).astype(jnp.float32)

    cos = cos_ref[...]
    sin = sin_ref[...]

    def rot(x, c, s):
        return x * c + pltpu.roll(x, HD // 2, 1) * s

    even = par_ref[0] == 0
    k2 = jnp.where(even, k2a[...], k2b[...])
    v2 = jnp.where(even, v2a[...], v2b[...])
    k = jnp.concatenate([k2, k1[...], k0[...]], 0).astype(jnp.float32)
    k = rot(k, cos, sin).astype(jnp.bfloat16)
    v = jnp.concatenate([v2, v1[...], v0[...]], 0)
    off = span - rows
    for a in range(tiles):
        lo = a * tile
        kk = k[lo:lo + band]
        vv = v[lo:lo + band]
        bias = bias_ref[a]
        qc = cos[off + lo:off + lo + tile]
        qs = sin[off + lo:off + lo + tile]
        for g in range(2):
            q = q_ref[lo:lo + tile, g * HD:(g + 1) * HD].astype(jnp.float32)
            q = rot(q, qc, qs).astype(jnp.bfloat16)
            s = lax.dot_general(q, kk, (((1,), (1,)), ((), ())), preferred_element_type=jnp.float32)
            s = s + bias
            m = jnp.max(s, axis=1, keepdims=True)
            w = jnp.exp2((s - m) * exp2_scale)
            tot = jnp.sum(w, axis=1, keepdims=True)
            pv = jnp.dot(w.astype(jnp.bfloat16), vv, preferred_element_type=jnp.float32)
            o_ref[lo:lo + tile, g * HD:(g + 1) * HD] = (pv / tot).astype(jnp.bfloat16)


def local(queries, keys, values, segment_ids):
    rows = queries.shape[0]
    hops = W // rows
    assert hops == 2
    span = (hops + 1) * rows
    shard = lax.axis_index("seq")
    count = lax.axis_size("seq")
    near = lax.ppermute((keys, values), "seq", [(s, s + 1) for s in range(count - 1)])
    far = lax.ppermute((keys, values), "seq", [(s, s + 2) for s in range(0, count - 2, 2)])
    seg_all = lax.all_gather(segment_ids, "seq", tiled=True)
    relay = lax.ppermute(near, "seq", [(s, s + 1) for s in range(0, count - 1, 2)])
    total = seg_all.shape[0]
    places = jnp.arange(total, dtype=jnp.int32)
    previous = jnp.concatenate([seg_all[:1], seg_all[:-1]])
    boundary = (seg_all != previous) | (places == 0)
    starts = lax.cummax(jnp.where(boundary, places, 0), axis=0)
    pos_all = jnp.concatenate([jnp.zeros((hops * rows,), jnp.int32), places - starts])
    pos_win = lax.dynamic_slice_in_dim(pos_all, shard * rows, span, 0)
    cos, sin = rope_tables(pos_win)
    pos_q = pos_win[span - rows:].reshape(rows, 1)
    parity = (shard % 2).astype(jnp.int32).reshape(1)
    kv_spec = pl.BlockSpec((rows, HD), lambda h, p: (0, h))
    full = lambda shape: pl.BlockSpec(shape, lambda h, p: (0, 0))
    tile = 256
    kernel = functools.partial(attend_kernel, rows=rows, hops=hops, tile=tile)
    heads = keys.shape[1] // HD
    grid_spec = pltpu.PrefetchScalarGridSpec(
        num_scalar_prefetch=1,
        grid=(heads,),
        in_specs=[full((rows, 1)), full((span, HD)), full((span, HD)),
                  pl.BlockSpec((rows, 2 * HD), lambda h, p: (0, h))] + [kv_spec] * 8,
        out_specs=pl.BlockSpec((rows, 2 * HD), lambda h, p: (0, h)),
        scratch_shapes=[pltpu.VMEM((rows // tile, tile, W + tile), jnp.float32)],
    )
    return pl.pallas_call(
        kernel,
        grid_spec=grid_spec,
        out_shape=jax.ShapeDtypeStruct(queries.shape, jnp.bfloat16),
        compiler_params=pltpu.CompilerParams(dimension_semantics=("arbitrary",)),
    )(parity, pos_q, cos, sin, queries, far[0], relay[0], near[0], keys,
      far[1], relay[1], near[1], values)


def solution(mesh):
    return jax.shard_map(
        local,
        mesh=mesh,
        in_specs=(
            P(("grp", "seq"), None),
            P(("grp", "seq"), None),
            P(("grp", "seq"), None),
            P(("grp", "seq")),
        ),
        out_specs=P(("grp", "seq"), None),
        check_vma=False,
    )
```

```python
import functools

import jax
import jax.numpy as jnp
from jax import lax
from jax.experimental import pallas as pl
from jax.experimental.pallas import tpu as pltpu
from jax.sharding import PartitionSpec as P

H = 32
KVH = 16
HD = 128
W = 1024


query_scale = 168.0 ** (-0.5)
exp2_scale = query_scale * 1.4426950408889634


def passed_along(value, axis, steps):
    count = lax.axis_size(axis)
    first, last = (max(0, -steps), min(count, count - steps))
    return lax.ppermute(value, axis, [(source, source + steps) for source in range(first, last)])


def rope_tables(doc_pos):
    half = HD // 2
    freqs = 10000.0 ** (-2.0 * jnp.arange(half, dtype=jnp.float32) / HD)
    angles = doc_pos.astype(jnp.float32)[:, None] * freqs[None, :]
    cos, sin = jnp.cos(angles), jnp.sin(angles)
    return jnp.concatenate([cos, cos], -1), jnp.concatenate([-sin, sin], -1)


def attend_kernel(par_ref, pos_ref, cos_ref, sin_ref, q_ref, *refs, rows, tile, first, final):
    if final:
        k2a, k2b, v2a, v2b, st_in, acc_in, o_ref, bias_ref = refs
    else:
        k1, k0, v1, v0, st_out, acc_out, bias_ref = refs
    tiles = rows // tile
    nkeys = bias_ref.shape[2]
    qoff = W

    def bounds(a):
        lo = max(0, a * tile - first)
        hi = min(nkeys, a * tile + W + tile - first)
        return lo, hi

    @pl.when(pl.program_id(0) == 0)
    def _():
        dp = pos_ref[...]
        for a in range(tiles):
            r = lax.broadcasted_iota(jnp.int32, (tile, nkeys), 0) + a * tile
            c = lax.broadcasted_iota(jnp.int32, (tile, nkeys), 1) + first
            gap = qoff + r - c
            vis = (gap >= 0) & (gap < W) & (gap <= dp[a * tile:(a + 1) * tile])
            bias_ref[a] = jnp.where(vis, 0.0, -1e30).astype(jnp.float32)

    cos = cos_ref[...]
    sin = sin_ref[...]

    def rot(x, c, s):
        return x * c + pltpu.roll(x, HD // 2, 1) * s

    if final:
        even = par_ref[0] == 0
        k = jnp.where(even, k2a[...], k2b[...])
        v = jnp.where(even, v2a[...], v2b[...])
    else:
        k = jnp.concatenate([k1[...], k0[...]], 0)
        v = jnp.concatenate([v1[...], v0[...]], 0)
    k = rot(k.astype(jnp.float32), cos[first:first + nkeys], sin[first:first + nkeys])
    k = k.astype(jnp.bfloat16)
    for a in range(tiles):
        lo, hi = bounds(a)
        r0 = a * tile
        kk = k[lo:hi]
        vv = v[lo:hi]
        bias = bias_ref[a, :, lo:hi]
        qc = cos[qoff + r0:qoff + r0 + tile]
        qs = sin[qoff + r0:qoff + r0 + tile]
        for g in range(2):
            cols = slice(g * HD, (g + 1) * HD)
            q = q_ref[r0:r0 + tile, cols].astype(jnp.float32)
            q = rot(q, qc, qs).astype(jnp.bfloat16)
            s = lax.dot_general(q, kk, (((1,), (1,)), ((), ())), preferred_element_type=jnp.float32)
            s = s + bias
            m = jnp.max(s, axis=1, keepdims=True)
            if final:
                m1 = st_in[0, r0:r0 + tile, g:g + 1]
                mm = jnp.maximum(m, m1)
                scale1 = jnp.exp2((m1 - mm) * exp2_scale)
                w = jnp.exp2((s - mm) * exp2_scale)
                tot = jnp.sum(w, axis=1, keepdims=True) + st_in[0, r0:r0 + tile, 2 + g:3 + g] * scale1
                pv = jnp.dot(w.astype(jnp.bfloat16), vv, preferred_element_type=jnp.float32)
                pv = pv + acc_in[r0:r0 + tile, cols] * scale1
                o_ref[r0:r0 + tile, cols] = (pv / tot).astype(jnp.bfloat16)
            else:
                w = jnp.exp2((s - m) * exp2_scale)
                st_out[0, r0:r0 + tile, g:g + 1] = m
                st_out[0, r0:r0 + tile, 2 + g:3 + g] = jnp.sum(w, axis=1, keepdims=True)
                acc_out[r0:r0 + tile, cols] = jnp.dot(
                    w.astype(jnp.bfloat16), vv, preferred_element_type=jnp.float32)


def local(queries, keys, values, segment_ids):
    rows = queries.shape[0]
    hops = W // rows
    assert hops == 2
    span = (hops + 1) * rows
    shard = lax.axis_index("seq")
    count = lax.axis_size("seq")
    near = lax.ppermute((keys, values), "seq", [(s, s + 1) for s in range(count - 1)])
    seg_all = lax.all_gather(segment_ids, "seq", tiled=True)
    keys_b, values_b, seg_all = lax.optimization_barrier((keys, values, seg_all))
    far = lax.ppermute((keys_b, values_b), "seq", [(s, s + 2) for s in range(0, count - 2, 2)])
    relay = lax.ppermute(near, "seq", [(s, s + 1) for s in range(0, count - 1, 2)])
    total = seg_all.shape[0]
    places = jnp.arange(total, dtype=jnp.int32)
    previous = jnp.concatenate([seg_all[:1], seg_all[:-1]])
    boundary = (seg_all != previous) | (places == 0)
    starts = lax.cummax(jnp.where(boundary, places, 0), axis=0)
    pos_all = jnp.concatenate([jnp.zeros((hops * rows,), jnp.int32), places - starts])
    pos_win = lax.dynamic_slice_in_dim(pos_all, shard * rows, span, 0)
    cos, sin = rope_tables(pos_win)
    pos_q = pos_win[span - rows:].reshape(rows, 1)
    parity = (shard % 2).astype(jnp.int32).reshape(1)
    tile = 256
    heads = keys.shape[1] // HD
    kv_spec = pl.BlockSpec((rows, HD), lambda h, p: (0, h))
    full = lambda shape: pl.BlockSpec(shape, lambda h, p: (0, 0))
    head_spec = pl.BlockSpec((rows, 2 * HD), lambda h, p: (0, h))
    stat_spec = pl.BlockSpec((1, rows, 128), lambda h, p: (h, 0, 0))
    lead = [full((rows, 1)), full((span, HD)), full((span, HD)), head_spec]
    params = pltpu.CompilerParams(dimension_semantics=("arbitrary",))
    f32 = jnp.float32
    stats, acc1 = pl.pallas_call(
        functools.partial(attend_kernel, rows=rows, tile=tile, first=rows, final=False),
        grid_spec=pltpu.PrefetchScalarGridSpec(
            num_scalar_prefetch=1, grid=(heads,),
            in_specs=lead + [kv_spec] * 4,
            out_specs=[stat_spec, head_spec],
            scratch_shapes=[pltpu.VMEM((rows // tile, tile, 2 * rows), f32)]),
        out_shape=[jax.ShapeDtypeStruct((heads, rows, 128), f32),
                   jax.ShapeDtypeStruct(queries.shape, f32)],
        compiler_params=params,
    )(parity, pos_q, cos, sin, queries, near[0], keys, near[1], values)
    return pl.pallas_call(
        functools.partial(attend_kernel, rows=rows, tile=tile, first=0, final=True),
        grid_spec=pltpu.PrefetchScalarGridSpec(
            num_scalar_prefetch=1, grid=(heads,),
            in_specs=lead + [kv_spec] * 4 + [stat_spec, head_spec],
            out_specs=head_spec,
            scratch_shapes=[pltpu.VMEM((rows // tile, tile, rows), f32)]),
        out_shape=jax.ShapeDtypeStruct(queries.shape, jnp.bfloat16),
        compiler_params=params,
    )(parity, pos_q, cos, sin, queries, far[0], relay[0], far[1], relay[1], stats, acc1)


def solution(mesh):
    return jax.shard_map(
        local,
        mesh=mesh,
        in_specs=(
            P(("grp", "seq"), None),
            P(("grp", "seq"), None),
            P(("grp", "seq"), None),
            P(("grp", "seq")),
        ),
        out_specs=P(("grp", "seq"), None),
        check_vma=False,
    )
```

```python
import functools

import jax
import jax.numpy as jnp
from jax import lax
from jax.experimental import pallas as pl
from jax.experimental.pallas import tpu as pltpu
from jax.sharding import PartitionSpec as P

H = 32
KVH = 16
HD = 128
W = 1024


query_scale = 168.0 ** (-0.5)
exp2_scale = query_scale * 1.4426950408889634


def passed_along(value, axis, steps):
    count = lax.axis_size(axis)
    first, last = (max(0, -steps), min(count, count - steps))
    return lax.ppermute(value, axis, [(source, source + steps) for source in range(first, last)])


def rope_tables(doc_pos):
    half = HD // 2
    freqs = 10000.0 ** (-2.0 * jnp.arange(half, dtype=jnp.float32) / HD)
    angles = doc_pos.astype(jnp.float32)[:, None] * freqs[None, :]
    cos, sin = jnp.cos(angles), jnp.sin(angles)
    return jnp.concatenate([cos, cos], -1), jnp.concatenate([-sin, sin], -1)


def attend_kernel(par_ref, pos_ref, cos_ref, sin_ref, q_ref, *refs, rows, tile, first, final):
    if final:
        k2a, k2b, v2a, v2b, st_in, acc_in, o_ref, bias_ref = refs
    else:
        k1, k0, v1, v0, st_out, acc_out, bias_ref = refs
    tiles = rows // tile
    nkeys = bias_ref.shape[2]
    qoff = W

    def bounds(a):
        lo = max(0, a * tile - first)
        hi = min(nkeys, a * tile + W + tile - first)
        return lo, hi

    @pl.when(pl.program_id(0) == 0)
    def _():
        dp = pos_ref[...]
        for a in range(tiles):
            r = lax.broadcasted_iota(jnp.int32, (tile, nkeys), 0) + a * tile
            c = lax.broadcasted_iota(jnp.int32, (tile, nkeys), 1) + first
            gap = qoff + r - c
            vis = (gap >= 0) & (gap < W) & (gap <= dp[a * tile:(a + 1) * tile])
            bias_ref[a] = jnp.where(vis, 0.0, -1e30).astype(jnp.float32)

    cos = cos_ref[...]
    sin = sin_ref[...]

    def rot(x, c, s):
        return x * c + pltpu.roll(x, HD // 2, 1) * s

    if final:
        even = par_ref[0] == 0
        k = jnp.where(even, k2a[...], k2b[...])
        v = jnp.where(even, v2a[...], v2b[...])
    else:
        k = jnp.concatenate([k1[...], k0[...]], 0)
        v = jnp.concatenate([v1[...], v0[...]], 0)
    k = rot(k.astype(jnp.float32), cos[first:first + nkeys], sin[first:first + nkeys])
    k = k.astype(jnp.bfloat16)
    lane = lax.broadcasted_iota(jnp.int32, (tile, 128), 1)
    for a in range(tiles):
        lo, hi = bounds(a)
        r0 = a * tile
        packed = []
        if final:
            st = st_in[0, r0:r0 + tile, :]
        kk = k[lo:hi]
        vv = v[lo:hi]
        bias = bias_ref[a, :, lo:hi]
        qc = cos[qoff + r0:qoff + r0 + tile]
        qs = sin[qoff + r0:qoff + r0 + tile]
        for g in range(2):
            cols = slice(g * HD, (g + 1) * HD)
            q = q_ref[r0:r0 + tile, cols].astype(jnp.float32)
            q = rot(q, qc, qs).astype(jnp.bfloat16)
            s = lax.dot_general(q, kk, (((1,), (1,)), ((), ())), preferred_element_type=jnp.float32)
            s = s + bias
            m = jnp.max(s, axis=1, keepdims=True)
            if final:
                m1 = jnp.max(jnp.where(lane == g, st, -3e38), axis=1, keepdims=True)
                l1 = jnp.max(jnp.where(lane == 2 + g, st, -3e38), axis=1, keepdims=True)
                mm = jnp.maximum(m, m1)
                scale1 = jnp.exp2((m1 - mm) * exp2_scale)
                w = jnp.exp2((s - mm) * exp2_scale)
                tot = jnp.sum(w, axis=1, keepdims=True) + l1 * scale1
                pv = jnp.dot(w.astype(jnp.bfloat16), vv, preferred_element_type=jnp.float32)
                pv = pv + acc_in[r0:r0 + tile, cols] * scale1
                o_ref[r0:r0 + tile, cols] = (pv / tot).astype(jnp.bfloat16)
            else:
                w = jnp.exp2((s - m) * exp2_scale)
                packed.append((m, jnp.sum(w, axis=1, keepdims=True)))
                acc_out[r0:r0 + tile, cols] = jnp.dot(
                    w.astype(jnp.bfloat16), vv, preferred_element_type=jnp.float32)
        if not final:
            (m0, l0), (m1_, l1_) = packed
            st = jnp.where(lane == 0, m0, jnp.where(lane == 1, m1_, jnp.where(lane == 2, l0, l1_)))
            st_out[0, r0:r0 + tile, :] = st


def local(queries, keys, values, segment_ids):
    rows = queries.shape[0]
    hops = W // rows
    assert hops == 2
    span = (hops + 1) * rows
    shard = lax.axis_index("seq")
    count = lax.axis_size("seq")
    near = lax.ppermute((keys, values), "seq", [(s, s + 1) for s in range(count - 1)])
    seg_all = lax.all_gather(segment_ids, "seq", tiled=True)
    keys_b, values_b, seg_all = lax.optimization_barrier((keys, values, seg_all))
    far = lax.ppermute((keys_b, values_b), "seq", [(s, s + 2) for s in range(0, count - 2, 2)])
    relay = lax.ppermute(near, "seq", [(s, s + 1) for s in range(0, count - 1, 2)])
    total = seg_all.shape[0]
    places = jnp.arange(total, dtype=jnp.int32)
    previous = jnp.concatenate([seg_all[:1], seg_all[:-1]])
    boundary = (seg_all != previous) | (places == 0)
    starts = lax.cummax(jnp.where(boundary, places, 0), axis=0)
    pos_all = jnp.concatenate([jnp.zeros((hops * rows,), jnp.int32), places - starts])
    pos_win = lax.dynamic_slice_in_dim(pos_all, shard * rows, span, 0)
    cos, sin = rope_tables(pos_win)
    pos_q = pos_win[span - rows:].reshape(rows, 1)
    parity = (shard % 2).astype(jnp.int32).reshape(1)
    tile = 256
    heads = keys.shape[1] // HD
    kv_spec = pl.BlockSpec((rows, HD), lambda h, p: (0, h))
    full = lambda shape: pl.BlockSpec(shape, lambda h, p: (0, 0))
    head_spec = pl.BlockSpec((rows, 2 * HD), lambda h, p: (0, h))
    stat_spec = pl.BlockSpec((1, rows, 128), lambda h, p: (h, 0, 0))
    lead = [full((rows, 1)), full((span, HD)), full((span, HD)), head_spec]
    params = pltpu.CompilerParams(dimension_semantics=("arbitrary",))
    f32 = jnp.float32
    stats, acc1 = pl.pallas_call(
        functools.partial(attend_kernel, rows=rows, tile=tile, first=rows, final=False),
        grid_spec=pltpu.PrefetchScalarGridSpec(
            num_scalar_prefetch=1, grid=(heads,),
            in_specs=lead + [kv_spec] * 4,
            out_specs=[stat_spec, head_spec],
            scratch_shapes=[pltpu.VMEM((rows // tile, tile, 2 * rows), f32)]),
        out_shape=[jax.ShapeDtypeStruct((heads, rows, 128), f32),
                   jax.ShapeDtypeStruct(queries.shape, f32)],
        compiler_params=params,
    )(parity, pos_q, cos, sin, queries, near[0], keys, near[1], values)
    return pl.pallas_call(
        functools.partial(attend_kernel, rows=rows, tile=tile, first=0, final=True),
        grid_spec=pltpu.PrefetchScalarGridSpec(
            num_scalar_prefetch=1, grid=(heads,),
            in_specs=lead + [kv_spec] * 4 + [stat_spec, head_spec],
            out_specs=head_spec,
            scratch_shapes=[pltpu.VMEM((rows // tile, tile, rows), f32)]),
        out_shape=jax.ShapeDtypeStruct(queries.shape, jnp.bfloat16),
        compiler_params=params,
    )(parity, pos_q, cos, sin, queries, far[0], relay[0], far[1], relay[1], stats, acc1)


def solution(mesh):
    return jax.shard_map(
        local,
        mesh=mesh,
        in_specs=(
            P(("grp", "seq"), None),
            P(("grp", "seq"), None),
            P(("grp", "seq"), None),
            P(("grp", "seq")),
        ),
        out_specs=P(("grp", "seq"), None),
        check_vma=False,
    )
```

```python
import functools

import jax
import jax.numpy as jnp
from jax import lax
from jax.experimental import pallas as pl
from jax.experimental.pallas import tpu as pltpu
from jax.sharding import PartitionSpec as P

H = 32
KVH = 16
HD = 128
W = 1024


query_scale = 168.0 ** (-0.5)
exp2_scale = query_scale * 1.4426950408889634


def passed_along(value, axis, steps):
    count = lax.axis_size(axis)
    first, last = (max(0, -steps), min(count, count - steps))
    return lax.ppermute(value, axis, [(source, source + steps) for source in range(first, last)])


def rope_tables(doc_pos):
    half = HD // 2
    freqs = 10000.0 ** (-2.0 * jnp.arange(half, dtype=jnp.float32) / HD)
    angles = doc_pos.astype(jnp.float32)[:, None] * freqs[None, :]
    cos, sin = jnp.cos(angles), jnp.sin(angles)
    return jnp.concatenate([cos, cos], -1), jnp.concatenate([-sin, sin], -1)


def attend_kernel(par_ref, pos_ref, cos_ref, sin_ref, q_ref, *refs, rows, tile, first, final):
    if final:
        k2a, k2b, v2a, v2b, st_in, acc_in, o_ref, bias_ref = refs
    else:
        k1, k0, v1, v0, st_out, acc_out, bias_ref = refs
    tiles = rows // tile
    nkeys = bias_ref.shape[2]
    qoff = W

    def bounds(a):
        lo = max(0, a * tile - first)
        hi = min(nkeys, a * tile + W + tile - first)
        return lo, hi

    @pl.when(pl.program_id(0) == 0)
    def _():
        dp = pos_ref[...]
        for a in range(tiles):
            r = lax.broadcasted_iota(jnp.int32, (tile, nkeys), 0) + a * tile
            c = lax.broadcasted_iota(jnp.int32, (tile, nkeys), 1) + first
            gap = qoff + r - c
            vis = (gap >= 0) & (gap < W) & (gap <= dp[a * tile:(a + 1) * tile])
            bias_ref[a] = jnp.where(vis, 0.0, -1e30).astype(jnp.float32)

    cos = cos_ref[...]
    sin = sin_ref[...]

    def rot(x, c, s):
        return x * c + pltpu.roll(x, HD // 2, 1) * s

    if final:
        even = par_ref[0] == 0
        k = jnp.where(even, k2a[...], k2b[...])
        v = jnp.where(even, v2a[...], v2b[...])
    else:
        k = jnp.concatenate([k1[...], k0[...]], 0)
        v = jnp.concatenate([v1[...], v0[...]], 0)
    k = rot(k.astype(jnp.float32), cos[first:first + nkeys], sin[first:first + nkeys])
    k = k.astype(jnp.bfloat16)
    lane = lax.broadcasted_iota(jnp.int32, (tile, 128), 1)
    for a in range(tiles):
        lo, hi = bounds(a)
        r0 = a * tile
        packed = []
        if final:
            st = st_in[0, r0:r0 + tile, :]
        kk = k[lo:hi]
        vv = v[lo:hi]
        bias = bias_ref[a, :, lo:hi]
        qc = cos[qoff + r0:qoff + r0 + tile]
        qs = sin[qoff + r0:qoff + r0 + tile]
        for g in range(2):
            cols = slice(g * HD, (g + 1) * HD)
            q = q_ref[r0:r0 + tile, cols].astype(jnp.float32)
            q = rot(q, qc, qs).astype(jnp.bfloat16)
            s = lax.dot_general(q, kk, (((1,), (1,)), ((), ())), preferred_element_type=jnp.float32)
            s = s + bias
            m = jnp.max(s, axis=1, keepdims=True)
            if final:
                m1 = jnp.max(jnp.where(lane == g, st, -3e38), axis=1, keepdims=True)
                l1 = jnp.max(jnp.where(lane == 2 + g, st, -3e38), axis=1, keepdims=True)
                mm = jnp.maximum(m, m1)
                scale1 = jnp.exp2((m1 - mm) * exp2_scale)
                w = jnp.exp2((s - mm) * exp2_scale)
                tot = jnp.sum(w, axis=1, keepdims=True) + l1 * scale1
                pv = jnp.dot(w.astype(jnp.bfloat16), vv, preferred_element_type=jnp.float32)
                pv = pv + acc_in[r0:r0 + tile, cols] * scale1
                o_ref[r0:r0 + tile, cols] = (pv / tot).astype(jnp.bfloat16)
            else:
                w = jnp.exp2((s - m) * exp2_scale)
                packed.append((m, jnp.sum(w, axis=1, keepdims=True)))
                acc_out[r0:r0 + tile, cols] = jnp.dot(
                    w.astype(jnp.bfloat16), vv, preferred_element_type=jnp.float32)
        if not final:
            (m0, l0), (m1_, l1_) = packed
            st = jnp.where(lane == 0, m0, jnp.where(lane == 1, m1_, jnp.where(lane == 2, l0, l1_)))
            st_out[0, r0:r0 + tile, :] = st


def local(queries, keys, values, segment_ids):
    rows = queries.shape[0]
    hops = W // rows
    assert hops == 2
    span = (hops + 1) * rows
    shard = lax.axis_index("seq")
    count = lax.axis_size("seq")
    both = jnp.concatenate([keys, values], 1)
    near = lax.ppermute(both, "seq", [(s, s + 1) for s in range(count - 1)])
    seg_all = lax.all_gather(segment_ids, "seq", tiled=True)
    both, seg_all = lax.optimization_barrier((both, seg_all))
    far = lax.ppermute(both, "seq", [(s, s + 2) for s in range(0, count - 2, 2)])
    relay = lax.ppermute(near, "seq", [(s, s + 1) for s in range(0, count - 1, 2)])
    total = seg_all.shape[0]
    places = jnp.arange(total, dtype=jnp.int32)
    previous = jnp.concatenate([seg_all[:1], seg_all[:-1]])
    boundary = (seg_all != previous) | (places == 0)
    starts = lax.cummax(jnp.where(boundary, places, 0), axis=0)
    pos_all = jnp.concatenate([jnp.zeros((hops * rows,), jnp.int32), places - starts])
    pos_win = lax.dynamic_slice_in_dim(pos_all, shard * rows, span, 0)
    cos, sin = rope_tables(pos_win)
    pos_q = pos_win[span - rows:].reshape(rows, 1)
    parity = (shard % 2).astype(jnp.int32).reshape(1)
    tile = 256
    heads = keys.shape[1] // HD
    kv_spec = pl.BlockSpec((rows, HD), lambda h, p: (0, h))
    v_spec = pl.BlockSpec((rows, HD), lambda h, p: (0, h + heads))
    full = lambda shape: pl.BlockSpec(shape, lambda h, p: (0, 0))
    head_spec = pl.BlockSpec((rows, 2 * HD), lambda h, p: (0, h))
    stat_spec = pl.BlockSpec((1, rows, 128), lambda h, p: (h, 0, 0))
    lead = [full((rows, 1)), full((span, HD)), full((span, HD)), head_spec]
    params = pltpu.CompilerParams(dimension_semantics=("arbitrary",))
    f32 = jnp.float32
    stats, acc1 = pl.pallas_call(
        functools.partial(attend_kernel, rows=rows, tile=tile, first=rows, final=False),
        grid_spec=pltpu.PrefetchScalarGridSpec(
            num_scalar_prefetch=1, grid=(heads,),
            in_specs=lead + [kv_spec, kv_spec, v_spec, kv_spec],
            out_specs=[stat_spec, head_spec],
            scratch_shapes=[pltpu.VMEM((rows // tile, tile, 2 * rows), f32)]),
        out_shape=[jax.ShapeDtypeStruct((heads, rows, 128), f32),
                   jax.ShapeDtypeStruct(queries.shape, f32)],
        compiler_params=params,
    )(parity, pos_q, cos, sin, queries, near, keys, near, values)
    return pl.pallas_call(
        functools.partial(attend_kernel, rows=rows, tile=tile, first=0, final=True),
        grid_spec=pltpu.PrefetchScalarGridSpec(
            num_scalar_prefetch=1, grid=(heads,),
            in_specs=lead + [kv_spec, kv_spec, v_spec, v_spec] + [stat_spec, head_spec],
            out_specs=head_spec,
            scratch_shapes=[pltpu.VMEM((rows // tile, tile, rows), f32)]),
        out_shape=jax.ShapeDtypeStruct(queries.shape, jnp.bfloat16),
        compiler_params=params,
    )(parity, pos_q, cos, sin, queries, far, relay, far, relay, stats, acc1)


def solution(mesh):
    return jax.shard_map(
        local,
        mesh=mesh,
        in_specs=(
            P(("grp", "seq"), None),
            P(("grp", "seq"), None),
            P(("grp", "seq"), None),
            P(("grp", "seq")),
        ),
        out_specs=P(("grp", "seq"), None),
        check_vma=False,
    )
```

```python
import functools

import jax
import jax.numpy as jnp
from jax import lax
from jax.experimental import pallas as pl
from jax.experimental.pallas import tpu as pltpu
from jax.sharding import PartitionSpec as P

H = 32
KVH = 16
HD = 128
W = 1024


query_scale = 168.0 ** (-0.5)
exp2_scale = query_scale * 1.4426950408889634


def passed_along(value, axis, steps):
    count = lax.axis_size(axis)
    first, last = (max(0, -steps), min(count, count - steps))
    return lax.ppermute(value, axis, [(source, source + steps) for source in range(first, last)])


def rope_tables(doc_pos):
    half = HD // 2
    freqs = 10000.0 ** (-2.0 * jnp.arange(half, dtype=jnp.float32) / HD)
    angles = doc_pos.astype(jnp.float32)[:, None] * freqs[None, :]
    cos, sin = jnp.cos(angles), jnp.sin(angles)
    return jnp.concatenate([cos, cos], -1), jnp.concatenate([-sin, sin], -1)


def attend_kernel(par_ref, pos_ref, cos_ref, sin_ref, q_ref, *refs, rows, tile, first, final):
    if final:
        k2a, k2b, v2a, v2b, st_in, acc_in, o_ref, bias_ref = refs
    else:
        k1, k0, v1, v0, st_out, acc_out, bias_ref = refs
    tiles = rows // tile
    nkeys = bias_ref.shape[2]
    qoff = W

    def bounds(a):
        lo = max(0, a * tile - first)
        hi = min(nkeys, a * tile + W + tile - first)
        return lo, hi

    @pl.when(pl.program_id(0) == 0)
    def _():
        dp = pos_ref[...]
        for a in range(tiles):
            r = lax.broadcasted_iota(jnp.int32, (tile, nkeys), 0) + a * tile
            c = lax.broadcasted_iota(jnp.int32, (tile, nkeys), 1) + first
            gap = qoff + r - c
            vis = (gap >= 0) & (gap < W) & (gap <= dp[a * tile:(a + 1) * tile])
            bias_ref[a] = jnp.where(vis, 0.0, -1e30).astype(jnp.float32)

    cos = cos_ref[...]
    sin = sin_ref[...]

    def rot(x, c, s):
        return x * c + pltpu.roll(x, HD // 2, 1) * s

    if final:
        even = par_ref[0] == 0
        k = jnp.where(even, k2a[...], k2b[...])
        v = jnp.where(even, v2a[...], v2b[...])
    else:
        k = jnp.concatenate([k1[...], k0[...]], 0)
        v = jnp.concatenate([v1[...], v0[...]], 0)
    k = rot(k.astype(jnp.float32), cos[first:first + nkeys], sin[first:first + nkeys])
    k = k.astype(jnp.bfloat16)
    lane = lax.broadcasted_iota(jnp.int32, (tile, 128), 1)
    for a in range(tiles):
        lo, hi = bounds(a)
        r0 = a * tile
        packed = []
        if final:
            st = st_in[0, r0:r0 + tile, :]
        kk = k[lo:hi]
        vv = v[lo:hi]
        bias = bias_ref[a, :, lo:hi]
        qc = cos[qoff + r0:qoff + r0 + tile]
        qs = sin[qoff + r0:qoff + r0 + tile]
        for g in range(2):
            cols = slice(g * HD, (g + 1) * HD)
            q = q_ref[r0:r0 + tile, cols].astype(jnp.float32)
            q = rot(q, qc, qs).astype(jnp.bfloat16)
            s = lax.dot_general(q, kk, (((1,), (1,)), ((), ())), preferred_element_type=jnp.float32)
            s = s + bias
            m = jnp.max(s, axis=1, keepdims=True)
            if final:
                m1 = jnp.max(jnp.where(lane == g, st, -3e38), axis=1, keepdims=True)
                l1 = jnp.max(jnp.where(lane == 2 + g, st, -3e38), axis=1, keepdims=True)
                mm = jnp.maximum(m, m1)
                scale1 = jnp.exp2((m1 - mm) * exp2_scale)
                w = jnp.exp2((s - mm) * exp2_scale)
                tot = jnp.sum(w, axis=1, keepdims=True) + l1 * scale1
                pv = jnp.dot(w.astype(jnp.bfloat16), vv, preferred_element_type=jnp.float32)
                pv = pv + acc_in[r0:r0 + tile, cols] * scale1
                o_ref[r0:r0 + tile, cols] = (pv / tot).astype(jnp.bfloat16)
            else:
                w = jnp.exp2((s - m) * exp2_scale)
                packed.append((m, jnp.sum(w, axis=1, keepdims=True)))
                acc_out[r0:r0 + tile, cols] = jnp.dot(
                    w.astype(jnp.bfloat16), vv, preferred_element_type=jnp.float32)
        if not final:
            (m0, l0), (m1_, l1_) = packed
            st = jnp.where(lane == 0, m0, jnp.where(lane == 1, m1_, jnp.where(lane == 2, l0, l1_)))
            st_out[0, r0:r0 + tile, :] = st


def local(queries, keys, values, segment_ids):
    rows = queries.shape[0]
    hops = W // rows
    assert hops == 2
    span = (hops + 1) * rows
    shard = lax.axis_index("seq")
    count = lax.axis_size("seq")
    seg_all = lax.all_gather(segment_ids, "seq", tiled=True)
    keys, values, seg_all = lax.optimization_barrier((keys, values, seg_all))
    both = jnp.concatenate([keys, values], 1)
    near = lax.ppermute(both, "seq", [(s, s + 1) for s in range(count - 1)])
    total = seg_all.shape[0]
    places = jnp.arange(total, dtype=jnp.int32)
    previous = jnp.concatenate([seg_all[:1], seg_all[:-1]])
    boundary = (seg_all != previous) | (places == 0)
    starts = lax.cummax(jnp.where(boundary, places, 0), axis=0)
    pos_all = jnp.concatenate([jnp.zeros((hops * rows,), jnp.int32), places - starts])
    pos_win = lax.dynamic_slice_in_dim(pos_all, shard * rows, span, 0)
    cos, sin = rope_tables(pos_win)
    pos_q = pos_win[span - rows:].reshape(rows, 1)
    parity = (shard % 2).astype(jnp.int32).reshape(1)
    both, near, cos, sin, pos_q = lax.optimization_barrier((both, near, cos, sin, pos_q))
    far = lax.ppermute(both, "seq", [(s, s + 2) for s in range(0, count - 2, 2)])
    relay = lax.ppermute(near, "seq", [(s, s + 1) for s in range(0, count - 1, 2)])
    tile = 256
    heads = keys.shape[1] // HD
    kv_spec = pl.BlockSpec((rows, HD), lambda h, p: (0, h))
    v_spec = pl.BlockSpec((rows, HD), lambda h, p: (0, h + heads))
    full = lambda shape: pl.BlockSpec(shape, lambda h, p: (0, 0))
    head_spec = pl.BlockSpec((rows, 2 * HD), lambda h, p: (0, h))
    stat_spec = pl.BlockSpec((1, rows, 128), lambda h, p: (h, 0, 0))
    lead = [full((rows, 1)), full((span, HD)), full((span, HD)), head_spec]
    params = pltpu.CompilerParams(dimension_semantics=("arbitrary",))
    f32 = jnp.float32
    stats, acc1 = pl.pallas_call(
        functools.partial(attend_kernel, rows=rows, tile=tile, first=rows, final=False),
        grid_spec=pltpu.PrefetchScalarGridSpec(
            num_scalar_prefetch=1, grid=(heads,),
            in_specs=lead + [kv_spec, kv_spec, v_spec, kv_spec],
            out_specs=[stat_spec, head_spec],
            scratch_shapes=[pltpu.VMEM((rows // tile, tile, 2 * rows), f32)]),
        out_shape=[jax.ShapeDtypeStruct((heads, rows, 128), f32),
                   jax.ShapeDtypeStruct(queries.shape, f32)],
        compiler_params=params,
    )(parity, pos_q, cos, sin, queries, near, keys, near, values)
    return pl.pallas_call(
        functools.partial(attend_kernel, rows=rows, tile=tile, first=0, final=True),
        grid_spec=pltpu.PrefetchScalarGridSpec(
            num_scalar_prefetch=1, grid=(heads,),
            in_specs=lead + [kv_spec, kv_spec, v_spec, v_spec] + [stat_spec, head_spec],
            out_specs=head_spec,
            scratch_shapes=[pltpu.VMEM((rows // tile, tile, rows), f32)]),
        out_shape=jax.ShapeDtypeStruct(queries.shape, jnp.bfloat16),
        compiler_params=params,
    )(parity, pos_q, cos, sin, queries, far, relay, far, relay, stats, acc1)


def solution(mesh):
    return jax.shard_map(
        local,
        mesh=mesh,
        in_specs=(
            P(("grp", "seq"), None),
            P(("grp", "seq"), None),
            P(("grp", "seq"), None),
            P(("grp", "seq")),
        ),
        out_specs=P(("grp", "seq"), None),
        check_vma=False,
    )
```

```python
import functools

import jax
import jax.numpy as jnp
from jax import lax
from jax.experimental import pallas as pl
from jax.experimental.pallas import tpu as pltpu
from jax.sharding import PartitionSpec as P

H = 32
KVH = 16
HD = 128
W = 1024


query_scale = 168.0 ** (-0.5)
exp2_scale = query_scale * 1.4426950408889634


def passed_along(value, axis, steps):
    count = lax.axis_size(axis)
    first, last = (max(0, -steps), min(count, count - steps))
    return lax.ppermute(value, axis, [(source, source + steps) for source in range(first, last)])


def rope_tables(doc_pos):
    half = HD // 2
    freqs = 10000.0 ** (-2.0 * jnp.arange(half, dtype=jnp.float32) / HD)
    angles = doc_pos.astype(jnp.float32)[:, None] * freqs[None, :]
    cos, sin = jnp.cos(angles), jnp.sin(angles)
    return jnp.concatenate([cos, cos], -1), jnp.concatenate([-sin, sin], -1)


def attend_kernel(par_ref, pos_ref, cos_ref, sin_ref, q_ref, *refs, rows, tile, first, final):
    if final:
        k2a, k2b, v2a, v2b, st_in, acc_in, o_ref, bias_ref = refs
    else:
        k1, k0, v1, v0, st_out, acc_out, bias_ref = refs
    tiles = rows // tile
    nkeys = bias_ref.shape[2]
    qoff = W

    def bounds(a):
        lo = max(0, a * tile - first)
        hi = min(nkeys, a * tile + W + tile - first)
        return lo, hi

    @pl.when(pl.program_id(0) == 0)
    def _():
        dp = pos_ref[...]
        for a in range(tiles):
            r = lax.broadcasted_iota(jnp.int32, (tile, nkeys), 0) + a * tile
            c = lax.broadcasted_iota(jnp.int32, (tile, nkeys), 1) + first
            gap = qoff + r - c
            vis = (gap >= 0) & (gap < W) & (gap <= dp[a * tile:(a + 1) * tile])
            bias_ref[a] = jnp.where(vis, 0.0, -1e30).astype(jnp.float32)

    cos = cos_ref[...]
    sin = sin_ref[...]

    def rot(x, c, s):
        return x * c + pltpu.roll(x, HD // 2, 1) * s

    if final:
        even = par_ref[0] == 0
        k = jnp.where(even, k2a[...], k2b[...])
        v = jnp.where(even, v2a[...], v2b[...])
    else:
        k = jnp.concatenate([k1[...], k0[...]], 0)
        v = jnp.concatenate([v1[...], v0[...]], 0)
    k = rot(k.astype(jnp.float32), cos[first:first + nkeys], sin[first:first + nkeys])
    k = k.astype(jnp.bfloat16)
    lane = lax.broadcasted_iota(jnp.int32, (tile, 128), 1)
    for a in range(tiles):
        lo, hi = bounds(a)
        r0 = a * tile
        packed = []
        if final:
            st = st_in[0, r0:r0 + tile, :]
        kk = k[lo:hi]
        vv = v[lo:hi]
        bias = bias_ref[a, :, lo:hi]
        qc = cos[qoff + r0:qoff + r0 + tile]
        qs = sin[qoff + r0:qoff + r0 + tile]
        for g in range(2):
            cols = slice(g * HD, (g + 1) * HD)
            q = q_ref[r0:r0 + tile, cols].astype(jnp.float32)
            q = rot(q, qc, qs).astype(jnp.bfloat16)
            s = lax.dot_general(q, kk, (((1,), (1,)), ((), ())), preferred_element_type=jnp.float32)
            s = s + bias
            m = jnp.max(s, axis=1, keepdims=True)
            if final:
                m1 = jnp.max(jnp.where(lane == g, st, -3e38), axis=1, keepdims=True)
                l1 = jnp.max(jnp.where(lane == 2 + g, st, -3e38), axis=1, keepdims=True)
                mm = jnp.maximum(m, m1)
                scale1 = jnp.exp2((m1 - mm) * exp2_scale)
                w = jnp.exp2((s - mm) * exp2_scale)
                tot = jnp.sum(w, axis=1, keepdims=True) + l1 * scale1
                pv = jnp.dot(w.astype(jnp.bfloat16), vv, preferred_element_type=jnp.float32)
                pv = pv + acc_in[r0:r0 + tile, cols] * scale1
                o_ref[r0:r0 + tile, cols] = (pv / tot).astype(jnp.bfloat16)
            else:
                w = jnp.exp2((s - m) * exp2_scale)
                packed.append((m, jnp.sum(w, axis=1, keepdims=True)))
                acc_out[r0:r0 + tile, cols] = jnp.dot(
                    w.astype(jnp.bfloat16), vv, preferred_element_type=jnp.float32)
        if not final:
            (m0, l0), (m1_, l1_) = packed
            st = jnp.where(lane == 0, m0, jnp.where(lane == 1, m1_, jnp.where(lane == 2, l0, l1_)))
            st_out[0, r0:r0 + tile, :] = st


def local(queries, keys, values, segment_ids):
    rows = queries.shape[0]
    hops = W // rows
    assert hops == 2
    span = (hops + 1) * rows
    shard = lax.axis_index("seq")
    count = lax.axis_size("seq")
    both = jnp.concatenate([keys, values], 1)
    near = lax.ppermute(both, "seq", [(s, s + 1) for s in range(count - 1)])
    placed = jnp.zeros((count, rows), jnp.int32).at[shard].set(segment_ids)
    seg_all = lax.psum(placed, "seq").reshape(count * rows)
    both, seg_all = lax.optimization_barrier((both, seg_all))
    far = lax.ppermute(both, "seq", [(s, s + 2) for s in range(0, count - 2, 2)])
    relay = lax.ppermute(near, "seq", [(s, s + 1) for s in range(0, count - 1, 2)])
    total = seg_all.shape[0]
    places = jnp.arange(total, dtype=jnp.int32)
    previous = jnp.concatenate([seg_all[:1], seg_all[:-1]])
    boundary = (seg_all != previous) | (places == 0)
    starts = lax.cummax(jnp.where(boundary, places, 0), axis=0)
    pos_all = jnp.concatenate([jnp.zeros((hops * rows,), jnp.int32), places - starts])
    pos_win = lax.dynamic_slice_in_dim(pos_all, shard * rows, span, 0)
    cos, sin = rope_tables(pos_win)
    pos_q = pos_win[span - rows:].reshape(rows, 1)
    parity = (shard % 2).astype(jnp.int32).reshape(1)
    tile = 256
    heads = keys.shape[1] // HD
    kv_spec = pl.BlockSpec((rows, HD), lambda h, p: (0, h))
    v_spec = pl.BlockSpec((rows, HD), lambda h, p: (0, h + heads))
    full = lambda shape: pl.BlockSpec(shape, lambda h, p: (0, 0))
    head_spec = pl.BlockSpec((rows, 2 * HD), lambda h, p: (0, h))
    stat_spec = pl.BlockSpec((1, rows, 128), lambda h, p: (h, 0, 0))
    lead = [full((rows, 1)), full((span, HD)), full((span, HD)), head_spec]
    params = pltpu.CompilerParams(dimension_semantics=("arbitrary",))
    f32 = jnp.float32
    stats, acc1 = pl.pallas_call(
        functools.partial(attend_kernel, rows=rows, tile=tile, first=rows, final=False),
        grid_spec=pltpu.PrefetchScalarGridSpec(
            num_scalar_prefetch=1, grid=(heads,),
            in_specs=lead + [kv_spec, kv_spec, v_spec, kv_spec],
            out_specs=[stat_spec, head_spec],
            scratch_shapes=[pltpu.VMEM((rows // tile, tile, 2 * rows), f32)]),
        out_shape=[jax.ShapeDtypeStruct((heads, rows, 128), f32),
                   jax.ShapeDtypeStruct(queries.shape, f32)],
        compiler_params=params,
    )(parity, pos_q, cos, sin, queries, near, keys, near, values)
    return pl.pallas_call(
        functools.partial(attend_kernel, rows=rows, tile=tile, first=0, final=True),
        grid_spec=pltpu.PrefetchScalarGridSpec(
            num_scalar_prefetch=1, grid=(heads,),
            in_specs=lead + [kv_spec, kv_spec, v_spec, v_spec] + [stat_spec, head_spec],
            out_specs=head_spec,
            scratch_shapes=[pltpu.VMEM((rows // tile, tile, rows), f32)]),
        out_shape=jax.ShapeDtypeStruct(queries.shape, jnp.bfloat16),
        compiler_params=params,
    )(parity, pos_q, cos, sin, queries, far, relay, far, relay, stats, acc1)


def solution(mesh):
    return jax.shard_map(
        local,
        mesh=mesh,
        in_specs=(
            P(("grp", "seq"), None),
            P(("grp", "seq"), None),
            P(("grp", "seq"), None),
            P(("grp", "seq")),
        ),
        out_specs=P(("grp", "seq"), None),
        check_vma=False,
    )
```

```python
import functools

import jax
import jax.numpy as jnp
from jax import lax
from jax.experimental import pallas as pl
from jax.experimental.pallas import tpu as pltpu
from jax.sharding import PartitionSpec as P

H = 32
KVH = 16
HD = 128
W = 1024


query_scale = 168.0 ** (-0.5)
exp2_scale = query_scale * 1.4426950408889634


def passed_along(value, axis, steps):
    count = lax.axis_size(axis)
    first, last = (max(0, -steps), min(count, count - steps))
    return lax.ppermute(value, axis, [(source, source + steps) for source in range(first, last)])


def rope_tables(doc_pos):
    half = HD // 2
    freqs = 10000.0 ** (-2.0 * jnp.arange(half, dtype=jnp.float32) / HD)
    angles = doc_pos.astype(jnp.float32)[:, None] * freqs[None, :]
    cos, sin = jnp.cos(angles), jnp.sin(angles)
    return jnp.concatenate([cos, cos], -1), jnp.concatenate([-sin, sin], -1)


def attend_kernel(par_ref, pos_ref, cos_ref, sin_ref, q_ref, *refs, rows, tile, first, final):
    if final:
        k2a, k2b, v2a, v2b, st_in, acc_in, o_ref, bias_ref = refs
    else:
        k1, k0, v1, v0, st_out, acc_out, bias_ref = refs
    tiles = rows // tile
    nkeys = bias_ref.shape[2]
    qoff = W

    def bounds(a):
        lo = max(0, a * tile - first)
        hi = min(nkeys, a * tile + W + tile - first)
        return lo, hi

    @pl.when(pl.program_id(0) == 0)
    def _():
        dp = pos_ref[...]
        for a in range(tiles):
            r = lax.broadcasted_iota(jnp.int32, (tile, nkeys), 0) + a * tile
            c = lax.broadcasted_iota(jnp.int32, (tile, nkeys), 1) + first
            gap = qoff + r - c
            vis = (gap >= 0) & (gap < W) & (gap <= dp[a * tile:(a + 1) * tile])
            bias_ref[a] = jnp.where(vis, 0.0, -1e30).astype(jnp.float32)

    cos = cos_ref[...]
    sin = sin_ref[...]

    def rot(x, c, s):
        return x * c + pltpu.roll(x, HD // 2, 1) * s

    if final:
        even = par_ref[0] == 0
        k = jnp.where(even, k2a[...], k2b[...])
        v = jnp.where(even, v2a[...], v2b[...])
    else:
        k = jnp.concatenate([k1[...], k0[...]], 0)
        v = jnp.concatenate([v1[...], v0[...]], 0)
    k = rot(k.astype(jnp.float32), cos[first:first + nkeys], sin[first:first + nkeys])
    k = k.astype(jnp.bfloat16)
    lane = lax.broadcasted_iota(jnp.int32, (tile, 128), 1)
    for a in range(tiles):
        lo, hi = bounds(a)
        r0 = a * tile
        packed = []
        if final:
            st = st_in[0, r0:r0 + tile, :]
        kk = k[lo:hi]
        vv = v[lo:hi]
        bias = bias_ref[a, :, lo:hi]
        qc = cos[qoff + r0:qoff + r0 + tile]
        qs = sin[qoff + r0:qoff + r0 + tile]
        for g in range(2):
            cols = slice(g * HD, (g + 1) * HD)
            q = q_ref[r0:r0 + tile, cols].astype(jnp.float32)
            q = rot(q, qc, qs).astype(jnp.bfloat16)
            s = lax.dot_general(q, kk, (((1,), (1,)), ((), ())), preferred_element_type=jnp.float32)
            s = s + bias
            m = jnp.max(s, axis=1, keepdims=True)
            if final:
                m1 = jnp.max(jnp.where(lane == g, st, -3e38), axis=1, keepdims=True)
                l1 = jnp.max(jnp.where(lane == 2 + g, st, -3e38), axis=1, keepdims=True)
                mm = jnp.maximum(m, m1)
                scale1 = jnp.exp2((m1 - mm) * exp2_scale)
                w = jnp.exp2((s - mm) * exp2_scale)
                tot = jnp.sum(w, axis=1, keepdims=True) + l1 * scale1
                pv = jnp.dot(w.astype(jnp.bfloat16), vv, preferred_element_type=jnp.float32)
                pv = pv + acc_in[r0:r0 + tile, cols] * scale1
                o_ref[r0:r0 + tile, cols] = (pv / tot).astype(jnp.bfloat16)
            else:
                w = jnp.exp2((s - m) * exp2_scale)
                packed.append((m, jnp.sum(w, axis=1, keepdims=True)))
                acc_out[r0:r0 + tile, cols] = jnp.dot(
                    w.astype(jnp.bfloat16), vv, preferred_element_type=jnp.float32)
        if not final:
            (m0, l0), (m1_, l1_) = packed
            st = jnp.where(lane == 0, m0, jnp.where(lane == 1, m1_, jnp.where(lane == 2, l0, l1_)))
            st_out[0, r0:r0 + tile, :] = st


def local(queries, keys, values, segment_ids):
    rows = queries.shape[0]
    hops = W // rows
    assert hops == 2
    span = (hops + 1) * rows
    shard = lax.axis_index("seq")
    count = lax.axis_size("seq")
    both = jnp.concatenate([keys, values], 1)
    near = lax.ppermute(both, "seq", [(s, s + 1) for s in range(count - 1)])
    seg_all = lax.all_gather(segment_ids, "seq", tiled=True)
    near, seg_all = lax.optimization_barrier((near, seg_all))
    far = lax.ppermute(near, "seq", [(s, s + 1) for s in range(count - 1)])
    total = seg_all.shape[0]
    places = jnp.arange(total, dtype=jnp.int32)
    previous = jnp.concatenate([seg_all[:1], seg_all[:-1]])
    boundary = (seg_all != previous) | (places == 0)
    starts = lax.cummax(jnp.where(boundary, places, 0), axis=0)
    pos_all = jnp.concatenate([jnp.zeros((hops * rows,), jnp.int32), places - starts])
    pos_win = lax.dynamic_slice_in_dim(pos_all, shard * rows, span, 0)
    cos, sin = rope_tables(pos_win)
    pos_q = pos_win[span - rows:].reshape(rows, 1)
    parity = (shard % 2).astype(jnp.int32).reshape(1)
    tile = 256
    heads = keys.shape[1] // HD
    kv_spec = pl.BlockSpec((rows, HD), lambda h, p: (0, h))
    v_spec = pl.BlockSpec((rows, HD), lambda h, p: (0, h + heads))
    full = lambda shape: pl.BlockSpec(shape, lambda h, p: (0, 0))
    head_spec = pl.BlockSpec((rows, 2 * HD), lambda h, p: (0, h))
    stat_spec = pl.BlockSpec((1, rows, 128), lambda h, p: (h, 0, 0))
    lead = [full((rows, 1)), full((span, HD)), full((span, HD)), head_spec]
    params = pltpu.CompilerParams(dimension_semantics=("arbitrary",))
    f32 = jnp.float32
    stats, acc1 = pl.pallas_call(
        functools.partial(attend_kernel, rows=rows, tile=tile, first=rows, final=False),
        grid_spec=pltpu.PrefetchScalarGridSpec(
            num_scalar_prefetch=1, grid=(heads,),
            in_specs=lead + [kv_spec, kv_spec, v_spec, kv_spec],
            out_specs=[stat_spec, head_spec],
            scratch_shapes=[pltpu.VMEM((rows // tile, tile, 2 * rows), f32)]),
        out_shape=[jax.ShapeDtypeStruct((heads, rows, 128), f32),
                   jax.ShapeDtypeStruct(queries.shape, f32)],
        compiler_params=params,
    )(parity, pos_q, cos, sin, queries, near, keys, near, values)
    return pl.pallas_call(
        functools.partial(attend_kernel, rows=rows, tile=tile, first=0, final=True),
        grid_spec=pltpu.PrefetchScalarGridSpec(
            num_scalar_prefetch=1, grid=(heads,),
            in_specs=lead + [kv_spec, kv_spec, v_spec, v_spec] + [stat_spec, head_spec],
            out_specs=head_spec,
            scratch_shapes=[pltpu.VMEM((rows // tile, tile, rows), f32)]),
        out_shape=jax.ShapeDtypeStruct(queries.shape, jnp.bfloat16),
        compiler_params=params,
    )(parity, pos_q, cos, sin, queries, far, far, far, far, stats, acc1)


def solution(mesh):
    return jax.shard_map(
        local,
        mesh=mesh,
        in_specs=(
            P(("grp", "seq"), None),
            P(("grp", "seq"), None),
            P(("grp", "seq"), None),
            P(("grp", "seq")),
        ),
        out_specs=P(("grp", "seq"), None),
        check_vma=False,
    )
```

```python
import functools

import jax
import jax.numpy as jnp
from jax import lax
from jax.experimental import pallas as pl
from jax.experimental.pallas import tpu as pltpu
from jax.sharding import PartitionSpec as P

H = 32
KVH = 16
HD = 128
W = 1024


query_scale = 168.0 ** (-0.5)
exp2_scale = query_scale * 1.4426950408889634


def passed_along(value, axis, steps):
    count = lax.axis_size(axis)
    first, last = (max(0, -steps), min(count, count - steps))
    return lax.ppermute(value, axis, [(source, source + steps) for source in range(first, last)])


def rope_tables(doc_pos):
    half = HD // 2
    freqs = 10000.0 ** (-2.0 * jnp.arange(half, dtype=jnp.float32) / HD)
    angles = doc_pos.astype(jnp.float32)[:, None] * freqs[None, :]
    cos, sin = jnp.cos(angles), jnp.sin(angles)
    return jnp.concatenate([cos, cos], -1), jnp.concatenate([-sin, sin], -1)


def attend_kernel(par_ref, pos_ref, cos_ref, sin_ref, q_ref, *refs, rows, tile, first, final):
    if final:
        k2a, k2b, v2a, v2b, st_in, acc_in, o_ref, bias_ref = refs
    else:
        k1, k0, v1, v0, st_out, acc_out, bias_ref = refs
    tiles = rows // tile
    nkeys = bias_ref.shape[2]
    qoff = W

    def bounds(a):
        lo = max(0, a * tile - first)
        hi = min(nkeys, a * tile + W + tile - first)
        return lo, hi

    @pl.when(pl.program_id(0) == 0)
    def _():
        dp = pos_ref[...]
        for a in range(tiles):
            r = lax.broadcasted_iota(jnp.int32, (tile, nkeys), 0) + a * tile
            c = lax.broadcasted_iota(jnp.int32, (tile, nkeys), 1) + first
            gap = qoff + r - c
            vis = (gap >= 0) & (gap < W) & (gap <= dp[a * tile:(a + 1) * tile])
            bias_ref[a] = jnp.where(vis, 0.0, -1e30).astype(jnp.float32)

    cos = cos_ref[...]
    sin = sin_ref[...]

    def rot(x, c, s):
        return x * c + pltpu.roll(x, HD // 2, 1) * s

    if final:
        even = par_ref[0] == 0
        k = jnp.where(even, k2a[...], k2b[...])
        v = jnp.where(even, v2a[...], v2b[...])
    else:
        k = jnp.concatenate([k1[...], k0[...]], 0)
        v = jnp.concatenate([v1[...], v0[...]], 0)
    k = rot(k.astype(jnp.float32), cos[first:first + nkeys], sin[first:first + nkeys])
    k = k.astype(jnp.bfloat16)
    lane = lax.broadcasted_iota(jnp.int32, (tile, 128), 1)
    for a in range(tiles):
        lo, hi = bounds(a)
        r0 = a * tile
        packed = []
        if final:
            st = st_in[0, r0:r0 + tile, :]
        kk = k[lo:hi]
        vv = v[lo:hi]
        bias = bias_ref[a, :, lo:hi]
        qc = cos[qoff + r0:qoff + r0 + tile]
        qs = sin[qoff + r0:qoff + r0 + tile]
        for g in range(2):
            cols = slice(g * HD, (g + 1) * HD)
            q = q_ref[r0:r0 + tile, cols].astype(jnp.float32)
            q = rot(q, qc, qs).astype(jnp.bfloat16)
            s = lax.dot_general(q, kk, (((1,), (1,)), ((), ())), preferred_element_type=jnp.float32)
            s = s + bias
            m = jnp.max(s, axis=1, keepdims=True)
            if final:
                m1 = jnp.max(jnp.where(lane == g, st, -3e38), axis=1, keepdims=True)
                l1 = jnp.max(jnp.where(lane == 2 + g, st, -3e38), axis=1, keepdims=True)
                mm = jnp.maximum(m, m1)
                scale1 = jnp.exp2((m1 - mm) * exp2_scale)
                w = jnp.exp2((s - mm) * exp2_scale)
                tot = jnp.sum(w, axis=1, keepdims=True) + l1 * scale1
                pv = jnp.dot(w.astype(jnp.bfloat16), vv, preferred_element_type=jnp.float32)
                pv = pv + acc_in[r0:r0 + tile, cols] * scale1
                o_ref[r0:r0 + tile, cols] = (pv / tot).astype(jnp.bfloat16)
            else:
                w = jnp.exp2((s - m) * exp2_scale)
                packed.append((m, jnp.sum(w, axis=1, keepdims=True)))
                acc_out[r0:r0 + tile, cols] = jnp.dot(
                    w.astype(jnp.bfloat16), vv, preferred_element_type=jnp.float32)
        if not final:
            (m0, l0), (m1_, l1_) = packed
            st = jnp.where(lane == 0, m0, jnp.where(lane == 1, m1_, jnp.where(lane == 2, l0, l1_)))
            st_out[0, r0:r0 + tile, :] = st


def local(queries, keys, values, segment_ids):
    rows = queries.shape[0]
    hops = W // rows
    assert hops == 2
    span = (hops + 1) * rows
    shard = lax.axis_index("seq")
    count = lax.axis_size("seq")
    pairs = [(s, s + 1) for s in range(count - 1)]
    near_k = lax.ppermute(keys, "seq", pairs)
    seg_all = lax.all_gather(segment_ids, "seq", tiled=True)
    values_b, seg_all = lax.optimization_barrier((values, seg_all))
    near_v = lax.ppermute(values_b, "seq", pairs)
    near = jnp.concatenate([near_k, near_v], 1)
    far = lax.ppermute(near, "seq", pairs)
    total = seg_all.shape[0]
    places = jnp.arange(total, dtype=jnp.int32)
    previous = jnp.concatenate([seg_all[:1], seg_all[:-1]])
    boundary = (seg_all != previous) | (places == 0)
    starts = lax.cummax(jnp.where(boundary, places, 0), axis=0)
    pos_all = jnp.concatenate([jnp.zeros((hops * rows,), jnp.int32), places - starts])
    pos_win = lax.dynamic_slice_in_dim(pos_all, shard * rows, span, 0)
    cos, sin = rope_tables(pos_win)
    pos_q = pos_win[span - rows:].reshape(rows, 1)
    parity = (shard % 2).astype(jnp.int32).reshape(1)
    tile = 256
    heads = keys.shape[1] // HD
    kv_spec = pl.BlockSpec((rows, HD), lambda h, p: (0, h))
    v_spec = pl.BlockSpec((rows, HD), lambda h, p: (0, h + heads))
    full = lambda shape: pl.BlockSpec(shape, lambda h, p: (0, 0))
    head_spec = pl.BlockSpec((rows, 2 * HD), lambda h, p: (0, h))
    stat_spec = pl.BlockSpec((1, rows, 128), lambda h, p: (h, 0, 0))
    lead = [full((rows, 1)), full((span, HD)), full((span, HD)), head_spec]
    params = pltpu.CompilerParams(dimension_semantics=("arbitrary",))
    f32 = jnp.float32
    stats, acc1 = pl.pallas_call(
        functools.partial(attend_kernel, rows=rows, tile=tile, first=rows, final=False),
        grid_spec=pltpu.PrefetchScalarGridSpec(
            num_scalar_prefetch=1, grid=(heads,),
            in_specs=lead + [kv_spec, kv_spec, v_spec, kv_spec],
            out_specs=[stat_spec, head_spec],
            scratch_shapes=[pltpu.VMEM((rows // tile, tile, 2 * rows), f32)]),
        out_shape=[jax.ShapeDtypeStruct((heads, rows, 128), f32),
                   jax.ShapeDtypeStruct(queries.shape, f32)],
        compiler_params=params,
    )(parity, pos_q, cos, sin, queries, near, keys, near, values)
    return pl.pallas_call(
        functools.partial(attend_kernel, rows=rows, tile=tile, first=0, final=True),
        grid_spec=pltpu.PrefetchScalarGridSpec(
            num_scalar_prefetch=1, grid=(heads,),
            in_specs=lead + [kv_spec, kv_spec, v_spec, v_spec] + [stat_spec, head_spec],
            out_specs=head_spec,
            scratch_shapes=[pltpu.VMEM((rows // tile, tile, rows), f32)]),
        out_shape=jax.ShapeDtypeStruct(queries.shape, jnp.bfloat16),
        compiler_params=params,
    )(parity, pos_q, cos, sin, queries, far, far, far, far, stats, acc1)


def solution(mesh):
    return jax.shard_map(
        local,
        mesh=mesh,
        in_specs=(
            P(("grp", "seq"), None),
            P(("grp", "seq"), None),
            P(("grp", "seq"), None),
            P(("grp", "seq")),
        ),
        out_specs=P(("grp", "seq"), None),
        check_vma=False,
    )
```

```python
import functools

import jax
import jax.numpy as jnp
from jax import lax
from jax.experimental import pallas as pl
from jax.experimental.pallas import tpu as pltpu
from jax.sharding import PartitionSpec as P


HD = 128
W = 1024


query_scale = 168.0 ** (-0.5)
exp2_scale = query_scale * 1.4426950408889634


def rope_tables(doc_pos):
    half = HD // 2
    freqs = 10000.0 ** (-2.0 * jnp.arange(half, dtype=jnp.float32) / HD)
    angles = doc_pos.astype(jnp.float32)[:, None] * freqs[None, :]
    cos, sin = jnp.cos(angles), jnp.sin(angles)
    return jnp.concatenate([cos, cos], -1), jnp.concatenate([-sin, sin], -1)


def attend_kernel(par_ref, pos_ref, cos_ref, sin_ref, q_ref, *refs, rows, tile, first, final):
    if final:
        k2a, k2b, v2a, v2b, st_in, acc_in, o_ref, bias_ref = refs
    else:
        k1, k0, v1, v0, st_out, acc_out, bias_ref = refs
    tiles = rows // tile
    nkeys = bias_ref.shape[2]
    qoff = W

    def bounds(a):
        lo = max(0, a * tile - first)
        hi = min(nkeys, a * tile + W + tile - first)
        return lo, hi

    @pl.when(pl.program_id(0) == 0)
    def _():
        dp = pos_ref[...]
        for a in range(tiles):
            r = lax.broadcasted_iota(jnp.int32, (tile, nkeys), 0) + a * tile
            c = lax.broadcasted_iota(jnp.int32, (tile, nkeys), 1) + first
            gap = qoff + r - c
            vis = (gap >= 0) & (gap < W) & (gap <= dp[a * tile:(a + 1) * tile])
            bias_ref[a] = jnp.where(vis, 0.0, -1e30).astype(jnp.float32)

    cos = cos_ref[...]
    sin = sin_ref[...]

    def rot(x, c, s):
        return x * c + pltpu.roll(x, HD // 2, 1) * s

    if final:
        even = par_ref[0] == 0
        k = jnp.where(even, k2a[...], k2b[...])
        v = jnp.where(even, v2a[...], v2b[...])
    else:
        k = jnp.concatenate([k1[...], k0[...]], 0)
        v = jnp.concatenate([v1[...], v0[...]], 0)
    k = rot(k.astype(jnp.float32), cos[first:first + nkeys], sin[first:first + nkeys])
    k = k.astype(jnp.bfloat16)
    lane = lax.broadcasted_iota(jnp.int32, (tile, 128), 1)
    for a in range(tiles):
        lo, hi = bounds(a)
        r0 = a * tile
        packed = []
        if final:
            st = st_in[0, r0:r0 + tile, :]
        kk = k[lo:hi]
        vv = v[lo:hi]
        bias = bias_ref[a, :, lo:hi]
        qc = cos[qoff + r0:qoff + r0 + tile]
        qs = sin[qoff + r0:qoff + r0 + tile]
        for g in range(2):
            cols = slice(g * HD, (g + 1) * HD)
            q = q_ref[r0:r0 + tile, cols].astype(jnp.float32)
            q = rot(q, qc, qs).astype(jnp.bfloat16)
            s = lax.dot_general(q, kk, (((1,), (1,)), ((), ())), preferred_element_type=jnp.float32)
            s = s + bias
            m = jnp.max(s, axis=1, keepdims=True)
            if final:
                m1 = jnp.max(jnp.where(lane == g, st, -3e38), axis=1, keepdims=True)
                l1 = jnp.max(jnp.where(lane == 2 + g, st, -3e38), axis=1, keepdims=True)
                mm = jnp.maximum(m, m1)
                scale1 = jnp.exp2((m1 - mm) * exp2_scale)
                w = jnp.exp2((s - mm) * exp2_scale)
                tot = jnp.sum(w, axis=1, keepdims=True) + l1 * scale1
                pv = jnp.dot(w.astype(jnp.bfloat16), vv, preferred_element_type=jnp.float32)
                pv = pv + acc_in[r0:r0 + tile, cols] * scale1
                o_ref[r0:r0 + tile, cols] = (pv / tot).astype(jnp.bfloat16)
            else:
                w = jnp.exp2((s - m) * exp2_scale)
                packed.append((m, jnp.sum(w, axis=1, keepdims=True)))
                acc_out[r0:r0 + tile, cols] = jnp.dot(
                    w.astype(jnp.bfloat16), vv, preferred_element_type=jnp.float32)
        if not final:
            (m0, l0), (m1_, l1_) = packed
            st = jnp.where(lane == 0, m0, jnp.where(lane == 1, m1_, jnp.where(lane == 2, l0, l1_)))
            st_out[0, r0:r0 + tile, :] = st


def local(queries, keys, values, segment_ids):
    rows = queries.shape[0]
    hops = W // rows
    assert hops == 2
    span = (hops + 1) * rows
    shard = lax.axis_index("seq")
    count = lax.axis_size("seq")
    pairs = [(s, s + 1) for s in range(count - 1)]
    near_k = lax.ppermute(keys, "seq", pairs)
    seg_all = lax.all_gather(segment_ids, "seq", tiled=True)
    values_b, seg_all = lax.optimization_barrier((values, seg_all))
    near_v = lax.ppermute(values_b, "seq", pairs)
    near = jnp.concatenate([near_k, near_v], 1)
    total = seg_all.shape[0]
    places = jnp.arange(total, dtype=jnp.int32)
    previous = jnp.concatenate([seg_all[:1], seg_all[:-1]])
    boundary = (seg_all != previous) | (places == 0)
    starts = lax.cummax(jnp.where(boundary, places, 0), axis=0)
    pos_all = jnp.concatenate([jnp.zeros((hops * rows,), jnp.int32), places - starts])
    pos_win = lax.dynamic_slice_in_dim(pos_all, shard * rows, span, 0)
    cos, sin = rope_tables(pos_win)
    pos_q = pos_win[span - rows:].reshape(rows, 1)
    parity = (shard % 2).astype(jnp.int32).reshape(1)
    near, cos, sin, pos_q = lax.optimization_barrier((near, cos, sin, pos_q))
    far = lax.ppermute(near, "seq", pairs)
    tile = 256
    heads = keys.shape[1] // HD
    kv_spec = pl.BlockSpec((rows, HD), lambda h, p: (0, h))
    v_spec = pl.BlockSpec((rows, HD), lambda h, p: (0, h + heads))
    full = lambda shape: pl.BlockSpec(shape, lambda h, p: (0, 0))
    head_spec = pl.BlockSpec((rows, 2 * HD), lambda h, p: (0, h))
    stat_spec = pl.BlockSpec((1, rows, 128), lambda h, p: (h, 0, 0))
    lead = [full((rows, 1)), full((span, HD)), full((span, HD)), head_spec]
    params = pltpu.CompilerParams(dimension_semantics=("arbitrary",))
    f32 = jnp.float32
    stats, acc1 = pl.pallas_call(
        functools.partial(attend_kernel, rows=rows, tile=tile, first=rows, final=False),
        grid_spec=pltpu.PrefetchScalarGridSpec(
            num_scalar_prefetch=1, grid=(heads,),
            in_specs=lead + [kv_spec, kv_spec, v_spec, kv_spec],
            out_specs=[stat_spec, head_spec],
            scratch_shapes=[pltpu.VMEM((rows // tile, tile, 2 * rows), f32)]),
        out_shape=[jax.ShapeDtypeStruct((heads, rows, 128), f32),
                   jax.ShapeDtypeStruct(queries.shape, f32)],
        compiler_params=params,
    )(parity, pos_q, cos, sin, queries, near, keys, near, values)
    return pl.pallas_call(
        functools.partial(attend_kernel, rows=rows, tile=tile, first=0, final=True),
        grid_spec=pltpu.PrefetchScalarGridSpec(
            num_scalar_prefetch=1, grid=(heads,),
            in_specs=lead + [kv_spec, kv_spec, v_spec, v_spec] + [stat_spec, head_spec],
            out_specs=head_spec,
            scratch_shapes=[pltpu.VMEM((rows // tile, tile, rows), f32)]),
        out_shape=jax.ShapeDtypeStruct(queries.shape, jnp.bfloat16),
        compiler_params=params,
    )(parity, pos_q, cos, sin, queries, far, far, far, far, stats, acc1)


def solution(mesh):
    return jax.shard_map(
        local,
        mesh=mesh,
        in_specs=(
            P(("grp", "seq"), None),
            P(("grp", "seq"), None),
            P(("grp", "seq"), None),
            P(("grp", "seq")),
        ),
        out_specs=P(("grp", "seq"), None),
        check_vma=False,
    )
```

```python
import functools

import jax
import jax.numpy as jnp
from jax import lax
from jax.experimental import pallas as pl
from jax.experimental.pallas import tpu as pltpu
from jax.sharding import PartitionSpec as P

H = 32
KVH = 16
HD = 128
W = 1024


query_scale = 168.0 ** (-0.5)
exp2_scale = query_scale * 1.4426950408889634


def passed_along(value, axis, steps):
    count = lax.axis_size(axis)
    first, last = (max(0, -steps), min(count, count - steps))
    return lax.ppermute(value, axis, [(source, source + steps) for source in range(first, last)])


def rope_tables(doc_pos):
    half = HD // 2
    freqs = 10000.0 ** (-2.0 * jnp.arange(half, dtype=jnp.float32) / HD)
    angles = doc_pos.astype(jnp.float32)[:, None] * freqs[None, :]
    cos, sin = jnp.cos(angles), jnp.sin(angles)
    return jnp.concatenate([cos, cos], -1), jnp.concatenate([-sin, sin], -1)


def attend_kernel(par_ref, pos_ref, cos_ref, sin_ref, q_ref, *refs, rows, tile, first, final):
    if final:
        k2, v2, st_in, acc_in, o_ref, bias_ref = refs
    else:
        k1, k0, v1, v0, st_out, acc_out, qr_out, bias_ref = refs
    tiles = rows // tile
    nkeys = bias_ref.shape[2]
    qoff = W

    def bounds(a):
        lo = max(0, a * tile - first)
        hi = min(nkeys, a * tile + W + tile - first)
        return lo, hi

    @pl.when(pl.program_id(0) == 0)
    def _():
        dp = pos_ref[...]
        for a in range(tiles):
            r = lax.broadcasted_iota(jnp.int32, (tile, nkeys), 0) + a * tile
            c = lax.broadcasted_iota(jnp.int32, (tile, nkeys), 1) + first
            gap = qoff + r - c
            vis = (gap >= 0) & (gap < W) & (gap <= dp[a * tile:(a + 1) * tile])
            bias_ref[a] = jnp.where(vis, 0.0, -1e30).astype(jnp.float32)

    cos = cos_ref[...]
    sin = sin_ref[...]

    def rot(x, c, s):
        return x * c + pltpu.roll(x, HD // 2, 1) * s

    if final:
        k = k2[...]
        v = v2[...]
    else:
        k = jnp.concatenate([k1[...], k0[...]], 0)
        v = jnp.concatenate([v1[...], v0[...]], 0)
    k = rot(k.astype(jnp.float32), cos[first:first + nkeys], sin[first:first + nkeys])
    k = k.astype(jnp.bfloat16)
    lane = lax.broadcasted_iota(jnp.int32, (tile, 128), 1)
    for a in range(tiles):
        lo, hi = bounds(a)
        r0 = a * tile
        packed = []
        if final:
            st = st_in[0, r0:r0 + tile, :]
        kk = k[lo:hi]
        vv = v[lo:hi]
        bias = bias_ref[a, :, lo:hi]
        qc = cos[qoff + r0:qoff + r0 + tile]
        qs = sin[qoff + r0:qoff + r0 + tile]
        for g in range(2):
            cols = slice(g * HD, (g + 1) * HD)
            if final:
                q = q_ref[r0:r0 + tile, cols]
            else:
                q = q_ref[r0:r0 + tile, cols].astype(jnp.float32)
                q = rot(q, qc, qs).astype(jnp.bfloat16)
                qr_out[r0:r0 + tile, cols] = q
            s = lax.dot_general(q, kk, (((1,), (1,)), ((), ())), preferred_element_type=jnp.float32)
            s = s + bias
            m = jnp.max(s, axis=1, keepdims=True)
            if final:
                m1 = jnp.max(jnp.where(lane == g, st, -3e38), axis=1, keepdims=True)
                l1 = jnp.max(jnp.where(lane == 2 + g, st, -3e38), axis=1, keepdims=True)
                mm = jnp.maximum(m, m1)
                scale1 = jnp.exp2((m1 - mm) * exp2_scale)
                w = jnp.exp2((s - mm) * exp2_scale)
                tot = jnp.sum(w, axis=1, keepdims=True) + l1 * scale1
                pv = jnp.dot(w.astype(jnp.bfloat16), vv, preferred_element_type=jnp.float32)
                pv = pv + acc_in[r0:r0 + tile, cols] * scale1
                o_ref[r0:r0 + tile, cols] = (pv / tot).astype(jnp.bfloat16)
            else:
                w = jnp.exp2((s - m) * exp2_scale)
                packed.append((m, jnp.sum(w, axis=1, keepdims=True)))
                acc_out[r0:r0 + tile, cols] = jnp.dot(
                    w.astype(jnp.bfloat16), vv, preferred_element_type=jnp.float32)
        if not final:
            (m0, l0), (m1_, l1_) = packed
            st = jnp.where(lane == 0, m0, jnp.where(lane == 1, m1_, jnp.where(lane == 2, l0, l1_)))
            st_out[0, r0:r0 + tile, :] = st


def local(queries, keys, values, segment_ids):
    rows = queries.shape[0]
    hops = W // rows
    assert hops == 2
    span = (hops + 1) * rows
    shard = lax.axis_index("seq")
    count = lax.axis_size("seq")
    both = jnp.concatenate([keys, values], 1)
    near = lax.ppermute(both, "seq", [(s, s + 1) for s in range(count - 1)])
    seg_all = lax.all_gather(segment_ids, "seq", tiled=True)
    near, seg_all = lax.optimization_barrier((near, seg_all))
    far = lax.ppermute(near, "seq", [(s, s + 1) for s in range(count - 1)])
    total = seg_all.shape[0]
    places = jnp.arange(total, dtype=jnp.int32)
    previous = jnp.concatenate([seg_all[:1], seg_all[:-1]])
    boundary = (seg_all != previous) | (places == 0)
    starts = lax.cummax(jnp.where(boundary, places, 0), axis=0)
    pos_all = jnp.concatenate([jnp.zeros((hops * rows,), jnp.int32), places - starts])
    pos_win = lax.dynamic_slice_in_dim(pos_all, shard * rows, span, 0)
    cos, sin = rope_tables(pos_win)
    pos_q = pos_win[span - rows:].reshape(rows, 1)
    parity = (shard % 2).astype(jnp.int32).reshape(1)
    tile = 256
    heads = keys.shape[1] // HD
    kv_spec = pl.BlockSpec((rows, HD), lambda h, p: (0, h))
    v_spec = pl.BlockSpec((rows, HD), lambda h, p: (0, h + heads))
    full = lambda shape: pl.BlockSpec(shape, lambda h, p: (0, 0))
    head_spec = pl.BlockSpec((rows, 2 * HD), lambda h, p: (0, h))
    stat_spec = pl.BlockSpec((1, rows, 128), lambda h, p: (h, 0, 0))
    lead = [full((rows, 1)), full((span, HD)), full((span, HD)), head_spec]
    params = pltpu.CompilerParams(dimension_semantics=("arbitrary",))
    f32 = jnp.float32
    stats, acc1, q_rot = pl.pallas_call(
        functools.partial(attend_kernel, rows=rows, tile=tile, first=rows, final=False),
        grid_spec=pltpu.PrefetchScalarGridSpec(
            num_scalar_prefetch=1, grid=(heads,),
            in_specs=lead + [kv_spec, kv_spec, v_spec, kv_spec],
            out_specs=[stat_spec, head_spec, head_spec],
            scratch_shapes=[pltpu.VMEM((rows // tile, tile, 2 * rows), f32)]),
        out_shape=[jax.ShapeDtypeStruct((heads, rows, 128), f32),
                   jax.ShapeDtypeStruct(queries.shape, f32),
                   jax.ShapeDtypeStruct(queries.shape, jnp.bfloat16)],
        compiler_params=params,
    )(parity, pos_q, cos, sin, queries, near, keys, near, values)
    return pl.pallas_call(
        functools.partial(attend_kernel, rows=rows, tile=tile, first=0, final=True),
        grid_spec=pltpu.PrefetchScalarGridSpec(
            num_scalar_prefetch=1, grid=(heads,),
            in_specs=lead + [kv_spec, v_spec] + [stat_spec, head_spec],
            out_specs=head_spec,
            scratch_shapes=[pltpu.VMEM((rows // tile, tile, rows), f32)]),
        out_shape=jax.ShapeDtypeStruct(queries.shape, jnp.bfloat16),
        compiler_params=params,
    )(parity, pos_q, cos, sin, q_rot, far, far, stats, acc1)


def solution(mesh):
    return jax.shard_map(
        local,
        mesh=mesh,
        in_specs=(
            P(("grp", "seq"), None),
            P(("grp", "seq"), None),
            P(("grp", "seq"), None),
            P(("grp", "seq")),
        ),
        out_specs=P(("grp", "seq"), None),
        check_vma=False,
    )
```

```python
import functools

import jax
import jax.numpy as jnp
from jax import lax
from jax.experimental import pallas as pl
from jax.experimental.pallas import tpu as pltpu
from jax.sharding import PartitionSpec as P

H = 32
KVH = 16
HD = 128
W = 1024


query_scale = 168.0 ** (-0.5)
exp2_scale = query_scale * 1.4426950408889634


def passed_along(value, axis, steps):
    count = lax.axis_size(axis)
    first, last = (max(0, -steps), min(count, count - steps))
    return lax.ppermute(value, axis, [(source, source + steps) for source in range(first, last)])


def rope_tables(doc_pos):
    half = HD // 2
    freqs = 10000.0 ** (-2.0 * jnp.arange(half, dtype=jnp.float32) / HD)
    angles = doc_pos.astype(jnp.float32)[:, None] * freqs[None, :]
    cos, sin = jnp.cos(angles), jnp.sin(angles)
    return jnp.concatenate([cos, cos], -1), jnp.concatenate([-sin, sin], -1)


def attend_kernel(par_ref, pos_ref, cos_ref, sin_ref, q_ref, *refs, rows, tile, first, final):
    if final:
        k2, v2, st_in, acc_in, o_ref, bias_ref = refs
    else:
        k1, k0, v1, v0, st_out, acc_out, qr_out, bias_ref = refs
    tiles = rows // tile
    nkeys = bias_ref.shape[2]
    qoff = W

    def bounds(a):
        lo = max(0, a * tile - first)
        hi = min(nkeys, a * tile + W + tile - first)
        return lo, hi

    @pl.when(pl.program_id(0) == 0)
    def _():
        dp = pos_ref[...]
        for a in range(tiles):
            r = lax.broadcasted_iota(jnp.int32, (tile, nkeys), 0) + a * tile
            c = lax.broadcasted_iota(jnp.int32, (tile, nkeys), 1) + first
            gap = qoff + r - c
            vis = (gap >= 0) & (gap < W) & (gap <= dp[a * tile:(a + 1) * tile])
            bias_ref[a] = jnp.where(vis, 0.0, -1e30).astype(jnp.float32)

    def rot(x, c, s):
        return x * c + pltpu.roll(x, HD // 2, 1) * s

    if final:
        k = k2[...]
        v = v2[...]
    else:
        k = jnp.concatenate([k1[...], k0[...]], 0)
        v = jnp.concatenate([v1[...], v0[...]], 0)
    k = rot(k.astype(jnp.float32), cos_ref[first:first + nkeys, :], sin_ref[first:first + nkeys, :])
    k = k.astype(jnp.bfloat16)
    lane = lax.broadcasted_iota(jnp.int32, (tile, 128), 1)
    for a in range(tiles):
        lo, hi = bounds(a)
        r0 = a * tile
        packed = []
        if final:
            st = st_in[0, r0:r0 + tile, :]
        kk = k[lo:hi]
        vv = v[lo:hi]
        bias = bias_ref[a, :, lo:hi]
        for g in range(2):
            cols = slice(g * HD, (g + 1) * HD)
            if final:
                q = q_ref[r0:r0 + tile, cols]
            else:
                q = q_ref[r0:r0 + tile, cols].astype(jnp.float32)
                qc = cos_ref[qoff + r0:qoff + r0 + tile, :]
                qs = sin_ref[qoff + r0:qoff + r0 + tile, :]
                q = rot(q, qc, qs).astype(jnp.bfloat16)
                qr_out[r0:r0 + tile, cols] = q
            s = lax.dot_general(q, kk, (((1,), (1,)), ((), ())), preferred_element_type=jnp.float32)
            s = s + bias
            m = jnp.max(s, axis=1, keepdims=True)
            if final:
                m1 = jnp.max(jnp.where(lane == g, st, -3e38), axis=1, keepdims=True)
                l1 = jnp.max(jnp.where(lane == 2 + g, st, -3e38), axis=1, keepdims=True)
                mm = jnp.maximum(m, m1)
                scale1 = jnp.exp2((m1 - mm) * exp2_scale)
                w = jnp.exp2((s - mm) * exp2_scale)
                tot = jnp.sum(w, axis=1, keepdims=True) + l1 * scale1
                pv = jnp.dot(w.astype(jnp.bfloat16), vv, preferred_element_type=jnp.float32)
                pv = pv + acc_in[r0:r0 + tile, cols] * scale1
                o_ref[r0:r0 + tile, cols] = (pv / tot).astype(jnp.bfloat16)
            else:
                w = jnp.exp2((s - m) * exp2_scale)
                packed.append((m, jnp.sum(w, axis=1, keepdims=True)))
                acc_out[r0:r0 + tile, cols] = jnp.dot(
                    w.astype(jnp.bfloat16), vv, preferred_element_type=jnp.float32)
        if not final:
            (m0, l0), (m1_, l1_) = packed
            st = jnp.where(lane == 0, m0, jnp.where(lane == 1, m1_, jnp.where(lane == 2, l0, l1_)))
            st_out[0, r0:r0 + tile, :] = st


def local(queries, keys, values, segment_ids):
    rows = queries.shape[0]
    hops = W // rows
    assert hops == 2
    span = (hops + 1) * rows
    shard = lax.axis_index("seq")
    count = lax.axis_size("seq")
    both = jnp.concatenate([keys, values], 1)
    near = lax.ppermute(both, "seq", [(s, s + 1) for s in range(count - 1)])
    seg_all = lax.all_gather(segment_ids, "seq", tiled=True)
    near, seg_all = lax.optimization_barrier((near, seg_all))
    far = lax.ppermute(near, "seq", [(s, s + 1) for s in range(count - 1)])
    total = seg_all.shape[0]
    places = jnp.arange(total, dtype=jnp.int32)
    previous = jnp.concatenate([seg_all[:1], seg_all[:-1]])
    boundary = (seg_all != previous) | (places == 0)
    starts = lax.cummax(jnp.where(boundary, places, 0), axis=0)
    pos_all = jnp.concatenate([jnp.zeros((hops * rows,), jnp.int32), places - starts])
    pos_win = lax.dynamic_slice_in_dim(pos_all, shard * rows, span, 0)
    cos, sin = rope_tables(pos_win)
    pos_q = pos_win[span - rows:].reshape(rows, 1)
    parity = (shard % 2).astype(jnp.int32).reshape(1)
    tile = 256
    heads = keys.shape[1] // HD
    kv_spec = pl.BlockSpec((rows, HD), lambda h, p: (0, h))
    v_spec = pl.BlockSpec((rows, HD), lambda h, p: (0, h + heads))
    full = lambda shape: pl.BlockSpec(shape, lambda h, p: (0, 0))
    head_spec = pl.BlockSpec((rows, 2 * HD), lambda h, p: (0, h))
    stat_spec = pl.BlockSpec((1, rows, 128), lambda h, p: (h, 0, 0))
    lead = [full((rows, 1)), full((span, HD)), full((span, HD)), head_spec]
    params = pltpu.CompilerParams(dimension_semantics=("arbitrary",))
    f32 = jnp.float32
    stats, acc1, q_rot = pl.pallas_call(
        functools.partial(attend_kernel, rows=rows, tile=tile, first=rows, final=False),
        grid_spec=pltpu.PrefetchScalarGridSpec(
            num_scalar_prefetch=1, grid=(heads,),
            in_specs=lead + [kv_spec, kv_spec, v_spec, kv_spec],
            out_specs=[stat_spec, head_spec, head_spec],
            scratch_shapes=[pltpu.VMEM((rows // tile, tile, 2 * rows), f32)]),
        out_shape=[jax.ShapeDtypeStruct((heads, rows, 128), f32),
                   jax.ShapeDtypeStruct(queries.shape, f32),
                   jax.ShapeDtypeStruct(queries.shape, jnp.bfloat16)],
        compiler_params=params,
    )(parity, pos_q, cos, sin, queries, near, keys, near, values)
    return pl.pallas_call(
        functools.partial(attend_kernel, rows=rows, tile=tile, first=0, final=True),
        grid_spec=pltpu.PrefetchScalarGridSpec(
            num_scalar_prefetch=1, grid=(heads,),
            in_specs=lead + [kv_spec, v_spec] + [stat_spec, head_spec],
            out_specs=head_spec,
            scratch_shapes=[pltpu.VMEM((rows // tile, tile, rows), f32)]),
        out_shape=jax.ShapeDtypeStruct(queries.shape, jnp.bfloat16),
        compiler_params=params,
    )(parity, pos_q, cos, sin, q_rot, far, far, stats, acc1)


def solution(mesh):
    return jax.shard_map(
        local,
        mesh=mesh,
        in_specs=(
            P(("grp", "seq"), None),
            P(("grp", "seq"), None),
            P(("grp", "seq"), None),
            P(("grp", "seq")),
        ),
        out_specs=P(("grp", "seq"), None),
        check_vma=False,
    )
```
